32 devices in a mesh: dp: 8 (over y, x, core), tensor: 4 (over z).
Axes of the slice: x: 2, y: 2, z: 4, core: 2. Of those that a mesh axis runs over, the one named last changes fastest.
Arguments:
- residual_in: bfloat16 [64, 2560], P(('dp', 'tensor')), may hold values from -6 to 6
- norm_gain: bfloat16 [2560], replicated, may hold values from 0.099609375 to 1.8984375
- w_query: bfloat16 [2560, 2560], P(None, 'tensor'), may hold values from -0.125 to 0.125
- key_weight: bfloat16 [2560, 640], P(None, 'tensor'), may hold values from -0.125 to 0.125
- value_weight: bfloat16 [2560, 640], P(None, 'tensor'), may hold values from -0.125 to 0.125
- key_page_pool: bfloat16 [256, 8, 80, 128], P('dp', 'tensor')
- value_page_pool: bfloat16 [256, 8, 80, 128], P('dp', 'tensor'), may hold values from -6 to 6
- lengths: int32 [64], replicated, may hold values from 1 to 512, as said below
- page_table: int32 [64, 4], replicated, may hold values from 0 to 255, as said below
- w_output: bfloat16 [2560, 2560], P('tensor'), may hold values from -0.125 to 0.125
- mlp_gain: bfloat16 [2560], replicated, may hold values from 0.099609375 to 1.8984375
- w_gate: bfloat16 [2560, 3584], P(None, 'tensor'), may hold values from -0.125 to 0.125
- w_up: bfloat16 [2560, 3584], P(None, 'tensor'), may hold values from -0.125 to 0.125
- w_down: bfloat16 [3584, 2560], P('tensor'), may hold values from -0.09375 to 0.09375
Outputs:
- residual_out: bfloat16 [64, 2560], P(('dp', 'tensor'))
The draws below stay inside these ranges and needn't reach their ends.
Inputs may be any that keep to these rules, and one draw needn't show every extreme that they name: `lengths`: every value from 1 to 512 can occur; 512 and 1 occur in every draw. `page_table`: all entries are distinct. Requests are ranked by lengths[r] * 64 + r, rising; rank k goes to serving index s = k % N where N = 8 is the number of indices of dp, or N - 1 - k % N when k // N is odd, as its (k // N)-th served request; all pages of a request lie in pool pages s * 32 to (s + 1) * 32 - 1 of its serving index; pages past a request's length hold unused data.
All inputs are finite; a program needn't handle non-finite values.
Results may differ from the reference program's by a relative error of at most 0.0096.
Values may be sent and summed in bfloat16 or wider, within the bound.
No kernel may reach another device: no remote copies, remote signals or barrier semaphores. Data moves between devices by JAX's collectives and lax.ppermute only.
A program may use at most 64 MiB of HBM per device.

```python
import jax
import jax.numpy as jnp
from jax import lax

MODEL_WIDTH = 2560
QUERY_HEADS = 32
KEY_VALUE_HEADS = 8
HEAD_SIZE = 80
FF = 3584
LONGEST_LENGTH = 512
PAGE_POSITIONS = 128
REQ_DEV = 8
REQUEST_COUNT = 64
PPR = 4
POOL = 32
POOL_PAGES = 256


def draw_key_page_pool(key, part):
    base_offset = jax.random.normal(jax.random.fold_in(key, 11), (POOL_PAGES, KEY_VALUE_HEADS, HEAD_SIZE, PAGE_POSITIONS), jnp.float32)
    return jnp.clip(base_offset, -6.0, 6.0).astype(jnp.bfloat16)


def common_lengths(key):
    value_rows = jax.random.randint(jax.random.fold_in(key, 21), (REQUEST_COUNT,), 1, LONGEST_LENGTH + 1)
    order = jax.random.permutation(jax.random.fold_in(key, 22), REQUEST_COUNT)
    value_rows = value_rows.at[order[0]].set(LONGEST_LENGTH)
    value_rows = value_rows.at[order[1]].set(1)
    return value_rows.astype(jnp.int32)


def draw_lengths(key, part):
    return common_lengths(key)


def draw_page_table(key, part):
    lengths = common_lengths(key)
    dp_count = REQUEST_COUNT // REQ_DEV
    ranking = lengths * REQUEST_COUNT + jnp.arange(REQUEST_COUNT, dtype=jnp.int32)
    order = jnp.argsort(ranking, stable=True)
    rank = jnp.argsort(order, stable=True).astype(jnp.int32)
    round_no = rank // dp_count
    column = rank % dp_count
    server = jnp.where(round_no % 2 == 0, column, dp_count - 1 - column)
    noise = jax.random.randint(jax.random.fold_in(key, 31), (dp_count, POOL), 0, 1048576)
    shuffled = jnp.argsort(noise * POOL + jnp.arange(POOL, dtype=jnp.int32)[None, :], axis=1, stable=True).astype(jnp.int32)
    local = round_no[:, None] * PPR + jnp.arange(PPR, dtype=jnp.int32)[None, :]
    picked = shuffled[server[:, None], local]
    return (server[:, None] * POOL + picked).astype(jnp.int32)


def steps_of(rng, dims, cuts, smallest, high):
    def one(axis_at, blocks):
        steps = jax.random.uniform(jax.random.fold_in(jax.random.fold_in(rng, 6), axis_at), (blocks,), jnp.float32, smallest / len(cuts), high / len(cuts))
        return jnp.repeat(jnp.exp(steps), dims[axis_at] // blocks).reshape((-1,) + (1,) * (len(dims) - axis_at - 1))

    loudness = one(*cuts[0])
    for cut in cuts[1:]:
        loudness = loudness * one(*cut)
    return loudness


def scatter_about(rng, extent, scale, bound, cuts=(), held_as=jnp.bfloat16):
    level = steps_of(rng, extent, cuts, -0.22, 0.18) if cuts else 1.0
    entries = jax.random.normal(rng, extent, jnp.float32) * scale * level
    return jnp.minimum(jnp.maximum(entries, -bound), bound).astype(held_as)


def setup_inputs(seed: int = 0) -> dict:
    key_list = jax.random.split(jax.random.key(seed), 15)
    return {
        "residual_in": scatter_about(key_list[0], (REQUEST_COUNT, MODEL_WIDTH), 1.0, 6.0, ((0, 32),)),
        "norm_gain": jnp.clip(1.0 + 0.18 * jax.random.normal(key_list[1], (MODEL_WIDTH,), jnp.float32), 0.099609375, 1.8984375).astype(jnp.bfloat16),
        "w_query": scatter_about(key_list[2], (MODEL_WIDTH, QUERY_HEADS * HEAD_SIZE), MODEL_WIDTH ** -0.5, 0.125, ((1, 4),)),
        "key_weight": scatter_about(key_list[3], (MODEL_WIDTH, KEY_VALUE_HEADS * HEAD_SIZE), MODEL_WIDTH ** -0.5, 0.125, ((1, 4),)),
        "value_weight": scatter_about(key_list[4], (MODEL_WIDTH, KEY_VALUE_HEADS * HEAD_SIZE), MODEL_WIDTH ** -0.5, 0.125, ((1, 4),)),
        "key_page_pool": draw_key_page_pool(jax.random.fold_in(key_list[14], 71), 0),
        "value_page_pool": scatter_about(key_list[6], (POOL_PAGES, KEY_VALUE_HEADS, HEAD_SIZE, PAGE_POSITIONS), 1.0, 6.0, ((0, 8), (1, 4))),
        "lengths": draw_lengths(jax.random.fold_in(key_list[14], 71), 0),
        "page_table": draw_page_table(jax.random.fold_in(key_list[14], 71), 0),
        "w_output": scatter_about(key_list[9], (QUERY_HEADS * HEAD_SIZE, MODEL_WIDTH), (QUERY_HEADS * HEAD_SIZE) ** -0.5, 0.125, ((0, 4),)),
        "mlp_gain": jnp.clip(1.0 + 0.18 * jax.random.normal(key_list[10], (MODEL_WIDTH,), jnp.float32), 0.099609375, 1.8984375).astype(jnp.bfloat16),
        "w_gate": scatter_about(key_list[11], (MODEL_WIDTH, FF), MODEL_WIDTH ** -0.5, 0.125, ((1, 4),)),
        "w_up": scatter_about(key_list[12], (MODEL_WIDTH, FF), MODEL_WIDTH ** -0.5, 0.125, ((1, 4),)),
        "w_down": scatter_about(key_list[13], (FF, MODEL_WIDTH), FF ** -0.5, 0.09375, ((0, 4),)),
    }


def norm_rows(value_rows, gain):
    value_rows = value_rows.astype(jnp.float32)
    return value_rows * lax.rsqrt(lax.optimization_barrier(jnp.mean(value_rows * value_rows, axis=-1, keepdims=True)) + 1e-05) * gain.astype(jnp.float32)

def apply_rotation(tensor, positions):
    half_dim = tensor.shape[-1] // 2
    inverse_freq = 1000000.0 ** (-(jnp.arange(half_dim, dtype=jnp.float32) * 2.0 / tensor.shape[-1]))
    angles = positions.astype(jnp.float32)[:, None] * inverse_freq[None, :]
    cosine = jnp.cos(angles)[:, None, :]
    sines = jnp.sin(angles)[:, None, :]
    first_half = tensor[..., :half_dim]
    second_half = tensor[..., half_dim:]
    return jnp.concatenate([first_half * cosine - second_half * sines, second_half * cosine + first_half * sines], axis=-1)

def reference(residual_in, norm_gain, w_query, key_weight, value_weight, key_page_pool, value_page_pool, lengths, page_table, w_output, mlp_gain, w_gate, w_up, w_down):
    group_width = QUERY_HEADS // KEY_VALUE_HEADS
    score_scale = 1.0 / HEAD_SIZE ** 0.5
    scaled_input = norm_rows(residual_in, norm_gain).astype(jnp.bfloat16)
    query_heads = apply_rotation(jnp.dot(scaled_input, w_query, preferred_element_type=jnp.float32).reshape(REQUEST_COUNT, QUERY_HEADS, HEAD_SIZE), lengths).astype(jnp.bfloat16)
    fresh_key = apply_rotation(jnp.dot(scaled_input, key_weight, preferred_element_type=jnp.float32).reshape(REQUEST_COUNT, KEY_VALUE_HEADS, HEAD_SIZE), lengths).astype(jnp.bfloat16)
    fresh_value = jnp.dot(scaled_input, value_weight, preferred_element_type=jnp.float32).astype(jnp.bfloat16).reshape(REQUEST_COUNT, KEY_VALUE_HEADS, HEAD_SIZE)

    def one_request(index_value):
        query_matrix = query_heads[index_value].astype(jnp.float32).reshape(KEY_VALUE_HEADS, group_width, HEAD_SIZE)
        page_list = page_table[index_value]
        key_rows = key_page_pool[page_list].astype(jnp.float32).transpose(1, 2, 0, 3).reshape(KEY_VALUE_HEADS, HEAD_SIZE, LONGEST_LENGTH)
        value_rows = value_page_pool[page_list].astype(jnp.float32).transpose(1, 2, 0, 3).reshape(KEY_VALUE_HEADS, HEAD_SIZE, LONGEST_LENGTH)
        scores = jnp.einsum('hgd,hdp->hgp', query_matrix, key_rows) * score_scale
        valid_pos = (jnp.arange(LONGEST_LENGTH, dtype=jnp.int32) < lengths[index_value])[None, None, :]
        own_score = jnp.einsum('hgd,hd->hg', query_matrix, fresh_key[index_value].astype(jnp.float32)) * score_scale
        best = jnp.maximum(lax.optimization_barrier(jnp.max(jnp.where(valid_pos, scores, -1e+30), axis=-1)), own_score)
        weights = jnp.where(valid_pos, jnp.exp(scores - best[..., None]), 0.0)
        own_weight = jnp.exp(own_score - best)
        numer = jnp.einsum('hgp,hdp->hgd', weights, value_rows) + own_weight[..., None] * fresh_value[index_value].astype(jnp.float32)[:, None, :]
        denom = lax.optimization_barrier(jnp.sum(weights, axis=-1)) + own_weight
        return (numer / denom[..., None]).reshape(QUERY_HEADS * HEAD_SIZE)
    attended = lax.map(one_request, jnp.arange(REQUEST_COUNT, dtype=jnp.int32)).astype(jnp.bfloat16)
    mixed = residual_in.astype(jnp.float32) + jnp.dot(attended, w_output, preferred_element_type=jnp.float32)
    normed_mlp = norm_rows(mixed, mlp_gain).astype(jnp.bfloat16)
    gate_act = jnp.dot(normed_mlp, w_gate, preferred_element_type=jnp.float32)
    up_act = jnp.dot(normed_mlp, w_up, preferred_element_type=jnp.float32)
    hidden = (jax.nn.silu(gate_act) * up_act).astype(jnp.bfloat16)
    return (mixed + jnp.dot(hidden, w_down, preferred_element_type=jnp.float32)).astype(jnp.bfloat16)
```

```python
import jax
import jax.numpy as jnp
from jax import lax
from jax.sharding import PartitionSpec as P

HEAD_SIZE = 80


def norm_rows(value_rows, gain):
    value_rows = value_rows.astype(jnp.float32)
    return (
        value_rows
        * lax.rsqrt(jnp.mean(value_rows * value_rows, axis=-1, keepdims=True) + 1e-05)
        * gain.astype(jnp.float32)
    )


def apply_rotation(tensor, positions):
    half_dim = tensor.shape[-1] // 2
    inverse_freq = 1000000.0 ** (
        -(jnp.arange(half_dim, dtype=jnp.float32) * 2.0 / tensor.shape[-1])
    )
    angles = positions.astype(jnp.float32)[:, None] * inverse_freq[None, :]
    cosine = jnp.cos(angles)[:, None, :]
    sines = jnp.sin(angles)[:, None, :]
    first_half = tensor[..., :half_dim]
    second_half = tensor[..., half_dim:]
    return jnp.concatenate(
        [first_half * cosine - second_half * sines, second_half * cosine + first_half * sines],
        axis=-1,
    )


def tensor_allreduce(part, tp_count):
    step = 1
    while step < tp_count:
        pairs = [(i, i ^ step) for i in range(tp_count)]
        part = part + lax.ppermute(part, "tensor", pairs)
        step *= 2
    return part


def local(
    residual_in,
    norm_gain,
    w_query,
    key_weight,
    value_weight,
    key_page_pool,
    value_page_pool,
    lengths,
    page_table,
    w_output,
    mlp_gain,
    w_gate,
    w_up,
    w_down,
):
    dp_count = lax.axis_size("dp")
    tp_count = lax.axis_size("tensor")
    rows_loc = residual_in.shape[0]
    req_loc = rows_loc * tp_count
    kv_loc = key_page_pool.shape[1]
    q_loc = w_query.shape[1] // HEAD_SIZE
    group_width = q_loc // kv_loc
    pool_size = key_page_pool.shape[0]
    page_len = key_page_pool.shape[3]
    per_req = page_table.shape[1]
    total_reqs = page_table.shape[0]
    score_scale = 1.0 / HEAD_SIZE**0.5
    dp_index = lax.axis_index("dp")
    tp_index = lax.axis_index("tensor")

    rows_all = lax.all_to_all(
        jnp.tile(residual_in, (dp_count * tp_count, 1)),
        ("dp", "tensor"),
        0,
        0,
        tiled=True,
    )

    request_ids = jnp.arange(total_reqs, dtype=jnp.int32)
    ranking = lengths * total_reqs + request_ids
    rank = jnp.sum((ranking[None, :] < ranking[:, None]).astype(jnp.int32), axis=1)
    round_no = rank // dp_count
    column = rank % dp_count
    server = jnp.where(round_no % 2 == 0, column, dp_count - 1 - column)
    slots = jnp.arange(req_loc, dtype=jnp.int32)
    hits = (server[None, :] == dp_index) & (round_no[None, :] == slots[:, None])
    served = jnp.sum(jnp.where(hits, request_ids[None, :], 0), axis=1)
    served_len = lengths[served]

    rows_srv = rows_all[served]
    scaled_input = norm_rows(rows_srv, norm_gain).astype(jnp.bfloat16)
    query_srv = (
        apply_rotation(
            jnp.dot(scaled_input, w_query, preferred_element_type=jnp.float32).reshape(
                req_loc, q_loc, HEAD_SIZE
            ),
            served_len,
        )
        .astype(jnp.bfloat16)
        .reshape(req_loc, kv_loc, group_width, HEAD_SIZE)
    )
    key_srv = apply_rotation(
        jnp.dot(scaled_input, key_weight, preferred_element_type=jnp.float32).reshape(
            req_loc, kv_loc, HEAD_SIZE
        ),
        served_len,
    ).astype(jnp.bfloat16)
    value_srv = (
        jnp.dot(scaled_input, value_weight, preferred_element_type=jnp.float32)
        .astype(jnp.bfloat16)
        .reshape(req_loc, kv_loc, HEAD_SIZE)
    )

    page_list = page_table[served] - dp_index * pool_size
    key_rows = key_page_pool[page_list]
    value_rows = value_page_pool[page_list]
    scores = (
        jnp.einsum("rhgd,rphdc->rhgpc", query_srv, key_rows, preferred_element_type=jnp.float32)
        * score_scale
    )
    positions = (
        jnp.arange(per_req, dtype=jnp.int32)[:, None] * page_len
        + jnp.arange(page_len, dtype=jnp.int32)[None, :]
    )
    valid_pos = (positions[None, :, :] < served_len[:, None, None])[:, None, None, :, :]
    own_score = (
        jnp.einsum("rhgd,rhd->rhg", query_srv, key_srv, preferred_element_type=jnp.float32)
        * score_scale
    )
    best = jnp.maximum(jnp.max(jnp.where(valid_pos, scores, -1e30), axis=(-2, -1)), own_score)
    weights = jnp.where(valid_pos, jnp.exp(scores - best[..., None, None]), 0.0)
    own_weight = jnp.exp(own_score - best)
    numer = (
        jnp.einsum("rhgpc,rphdc->rhgd", weights, value_rows.astype(jnp.float32))
        + own_weight[..., None] * value_srv.astype(jnp.float32)[:, :, None, :]
    )
    denom = jnp.sum(weights, axis=(-2, -1)) + own_weight
    attended = (numer / denom[..., None]).reshape(req_loc, q_loc * HEAD_SIZE).astype(jnp.bfloat16)

    summed = tensor_allreduce(
        jnp.dot(attended, w_output, preferred_element_type=jnp.float32), tp_count
    )
    mixed = rows_srv.astype(jnp.float32) + summed
    normed_mlp = norm_rows(mixed, mlp_gain).astype(jnp.bfloat16)
    gate_act = jnp.dot(normed_mlp, w_gate, preferred_element_type=jnp.float32)
    up_act = jnp.dot(normed_mlp, w_up, preferred_element_type=jnp.float32)
    hidden = (jax.nn.silu(gate_act) * up_act).astype(jnp.bfloat16)
    down_sum = tensor_allreduce(
        jnp.dot(hidden, w_down, preferred_element_type=jnp.float32), tp_count
    )
    final = (mixed + down_sum).astype(jnp.bfloat16)

    dest_rows = (
        jnp.arange(dp_count, dtype=jnp.int32)[:, None] * req_loc
        + tp_index * rows_loc
        + jnp.arange(rows_loc, dtype=jnp.int32)[None, :]
    ).reshape(-1)
    outgoing = final[round_no[dest_rows]]
    incoming = lax.all_to_all(outgoing, "dp", 0, 0, tiled=True)
    mine = dp_index * req_loc + tp_index * rows_loc + jnp.arange(rows_loc, dtype=jnp.int32)
    pick = server[mine] * rows_loc + jnp.arange(rows_loc, dtype=jnp.int32)
    return incoming[pick]


def solution(mesh):
    return jax.shard_map(
        local,
        mesh=mesh,
        in_specs=(
            P(("dp", "tensor"), None),
            P(),
            P(None, "tensor"),
            P(None, "tensor"),
            P(None, "tensor"),
            P("dp", "tensor", None, None),
            P("dp", "tensor", None, None),
            P(),
            P(),
            P("tensor", None),
            P(),
            P(None, "tensor"),
            P(None, "tensor"),
            P("tensor", None),
        ),
        out_specs=P(("dp", "tensor"), None),
        check_vma=False,
    )
```

```python
import jax
import jax.numpy as jnp
from jax import lax
from jax.sharding import PartitionSpec as P

HEAD_SIZE = 80


def norm_rows(value_rows, gain):
    value_rows = value_rows.astype(jnp.float32)
    return (
        value_rows
        * lax.rsqrt(jnp.mean(value_rows * value_rows, axis=-1, keepdims=True) + 1e-05)
        * gain.astype(jnp.float32)
    )


def apply_rotation(tensor, positions):
    half_dim = tensor.shape[-1] // 2
    inverse_freq = 1000000.0 ** (
        -(jnp.arange(half_dim, dtype=jnp.float32) * 2.0 / tensor.shape[-1])
    )
    angles = positions.astype(jnp.float32)[:, None] * inverse_freq[None, :]
    cosine = jnp.cos(angles)[:, None, :]
    sines = jnp.sin(angles)[:, None, :]
    first_half = tensor[..., :half_dim]
    second_half = tensor[..., half_dim:]
    return jnp.concatenate(
        [first_half * cosine - second_half * sines, second_half * cosine + first_half * sines],
        axis=-1,
    )


def tensor_allreduce(part, tp_count):
    step = 1
    while step < tp_count:
        pairs = [(i, i ^ step) for i in range(tp_count)]
        part = part + lax.ppermute(part, "tensor", pairs)
        step *= 2
    return part


def local(
    residual_in,
    norm_gain,
    w_query,
    key_weight,
    value_weight,
    key_page_pool,
    value_page_pool,
    lengths,
    page_table,
    w_output,
    mlp_gain,
    w_gate,
    w_up,
    w_down,
):
    dp_count = lax.axis_size("dp")
    tp_count = lax.axis_size("tensor")
    rows_loc = residual_in.shape[0]
    req_loc = rows_loc * tp_count
    kv_loc = key_page_pool.shape[1]
    q_loc = w_query.shape[1] // HEAD_SIZE
    group_width = q_loc // kv_loc
    pool_size = key_page_pool.shape[0]
    page_len = key_page_pool.shape[3]
    per_req = page_table.shape[1]
    total_reqs = page_table.shape[0]
    score_scale = 1.0 / HEAD_SIZE**0.5
    dp_index = lax.axis_index("dp")
    tp_index = lax.axis_index("tensor")

    width = residual_in.shape[1]
    dev_count = dp_count * tp_count
    packed = residual_in.reshape(1, rows_loc * width)
    rows_all = lax.all_to_all(
        jnp.broadcast_to(packed, (dev_count, rows_loc * width)),
        ("dp", "tensor"),
        0,
        0,
        tiled=True,
    )

    request_ids = jnp.arange(total_reqs, dtype=jnp.int32)
    ranking = lengths * total_reqs + request_ids
    rank = jnp.sum((ranking[None, :] < ranking[:, None]).astype(jnp.int32), axis=1)
    round_no = rank // dp_count
    column = rank % dp_count
    server = jnp.where(round_no % 2 == 0, column, dp_count - 1 - column)
    slots = jnp.arange(req_loc, dtype=jnp.int32)
    hits = (server[None, :] == dp_index) & (round_no[None, :] == slots[:, None])
    served = jnp.sum(jnp.where(hits, request_ids[None, :], 0), axis=1)
    served_len = lengths[served]

    src_hot = (served[:, None] // rows_loc == jnp.arange(dev_count, dtype=jnp.int32)[None, :])
    picked = jnp.dot(src_hot.astype(jnp.bfloat16), rows_all, preferred_element_type=jnp.float32)
    picked = picked.reshape(req_loc, rows_loc, width)
    seg_hot = served[:, None] % rows_loc == jnp.arange(rows_loc, dtype=jnp.int32)[None, :]
    rows_srv = jnp.sum(jnp.where(seg_hot[:, :, None], picked, 0.0), axis=1).astype(jnp.bfloat16)
    scaled_input = norm_rows(rows_srv, norm_gain).astype(jnp.bfloat16)
    query_srv = (
        apply_rotation(
            jnp.dot(scaled_input, w_query, preferred_element_type=jnp.float32).reshape(
                req_loc, q_loc, HEAD_SIZE
            ),
            served_len,
        )
        .astype(jnp.bfloat16)
        .reshape(req_loc, kv_loc, group_width, HEAD_SIZE)
    )
    key_srv = apply_rotation(
        jnp.dot(scaled_input, key_weight, preferred_element_type=jnp.float32).reshape(
            req_loc, kv_loc, HEAD_SIZE
        ),
        served_len,
    ).astype(jnp.bfloat16)
    value_srv = (
        jnp.dot(scaled_input, value_weight, preferred_element_type=jnp.float32)
        .astype(jnp.bfloat16)
        .reshape(req_loc, kv_loc, HEAD_SIZE)
    )

    page_list = page_table[served] - dp_index * pool_size
    key_rows = key_page_pool[page_list]
    value_rows = value_page_pool[page_list]
    scores = (
        jnp.einsum("rhgd,rphdc->rhgpc", query_srv, key_rows, preferred_element_type=jnp.float32)
        * score_scale
    )
    positions = (
        jnp.arange(per_req, dtype=jnp.int32)[:, None] * page_len
        + jnp.arange(page_len, dtype=jnp.int32)[None, :]
    )
    valid_pos = (positions[None, :, :] < served_len[:, None, None])[:, None, None, :, :]
    own_score = (
        jnp.einsum("rhgd,rhd->rhg", query_srv, key_srv, preferred_element_type=jnp.float32)
        * score_scale
    )
    best = jnp.maximum(jnp.max(jnp.where(valid_pos, scores, -1e30), axis=(-2, -1)), own_score)
    weights = jnp.where(valid_pos, jnp.exp(scores - best[..., None, None]), 0.0)
    own_weight = jnp.exp(own_score - best)
    numer = (
        jnp.einsum("rhgpc,rphdc->rhgd", weights, value_rows.astype(jnp.float32))
        + own_weight[..., None] * value_srv.astype(jnp.float32)[:, :, None, :]
    )
    denom = jnp.sum(weights, axis=(-2, -1)) + own_weight
    attended = (numer / denom[..., None]).reshape(req_loc, q_loc * HEAD_SIZE).astype(jnp.bfloat16)

    summed = tensor_allreduce(
        jnp.dot(attended, w_output, preferred_element_type=jnp.float32), tp_count
    )
    mixed = rows_srv.astype(jnp.float32) + summed
    normed_mlp = norm_rows(mixed, mlp_gain).astype(jnp.bfloat16)
    gate_act = jnp.dot(normed_mlp, w_gate, preferred_element_type=jnp.float32)
    up_act = jnp.dot(normed_mlp, w_up, preferred_element_type=jnp.float32)
    hidden = (jax.nn.silu(gate_act) * up_act).astype(jnp.bfloat16)
    down_sum = tensor_allreduce(
        jnp.dot(hidden, w_down, preferred_element_type=jnp.float32), tp_count
    )
    final = (mixed + down_sum).astype(jnp.bfloat16)

    dest_rows = (
        jnp.arange(dp_count, dtype=jnp.int32)[:, None] * req_loc
        + tp_index * rows_loc
        + jnp.arange(rows_loc, dtype=jnp.int32)[None, :]
    ).reshape(-1)
    out_hot = round_no[dest_rows][:, None] == slots[None, :]
    outgoing = jnp.dot(
        out_hot.astype(jnp.bfloat16), final, preferred_element_type=jnp.float32
    ).astype(jnp.bfloat16)
    incoming = lax.all_to_all(outgoing, "dp", 0, 0, tiled=True)
    mine = dp_index * req_loc + tp_index * rows_loc + jnp.arange(rows_loc, dtype=jnp.int32)
    pick = server[mine] * rows_loc + jnp.arange(rows_loc, dtype=jnp.int32)
    in_hot = pick[:, None] == jnp.arange(dp_count * rows_loc, dtype=jnp.int32)[None, :]
    return jnp.dot(
        in_hot.astype(jnp.bfloat16), incoming, preferred_element_type=jnp.float32
    ).astype(jnp.bfloat16)


def solution(mesh):
    return jax.shard_map(
        local,
        mesh=mesh,
        in_specs=(
            P(("dp", "tensor"), None),
            P(),
            P(None, "tensor"),
            P(None, "tensor"),
            P(None, "tensor"),
            P("dp", "tensor", None, None),
            P("dp", "tensor", None, None),
            P(),
            P(),
            P("tensor", None),
            P(),
            P(None, "tensor"),
            P(None, "tensor"),
            P("tensor", None),
        ),
        out_specs=P(("dp", "tensor"), None),
        check_vma=False,
    )
```

```python
import jax
import jax.numpy as jnp
from jax import lax
from jax.experimental import pallas as pl
from jax.experimental.pallas import tpu as pltpu
from jax.sharding import PartitionSpec as P

HEAD_SIZE = 80


def norm_rows(value_rows, gain):
    value_rows = value_rows.astype(jnp.float32)
    return (
        value_rows
        * lax.rsqrt(jnp.mean(value_rows * value_rows, axis=-1, keepdims=True) + 1e-05)
        * gain.astype(jnp.float32)
    )


def apply_rotation(tensor, positions):
    half_dim = tensor.shape[-1] // 2
    inverse_freq = 1000000.0 ** (
        -(jnp.arange(half_dim, dtype=jnp.float32) * 2.0 / tensor.shape[-1])
    )
    angles = positions.astype(jnp.float32)[:, None] * inverse_freq[None, :]
    cosine = jnp.cos(angles)[:, None, :]
    sines = jnp.sin(angles)[:, None, :]
    first_half = tensor[..., :half_dim]
    second_half = tensor[..., half_dim:]
    return jnp.concatenate(
        [first_half * cosine - second_half * sines, second_half * cosine + first_half * sines],
        axis=-1,
    )


def _contract_k_kernel(x_ref, *refs):
    count = len(refs) // 2
    w_refs, o_refs = refs[:count], refs[count:]

    @pl.when(pl.program_id(0) == 0)
    def _():
        for o_ref in o_refs:
            o_ref[...] = jnp.zeros_like(o_ref)

    x = x_ref[...]
    for w_ref, o_ref in zip(w_refs, o_refs):
        o_ref[...] += jnp.dot(x, w_ref[...], preferred_element_type=jnp.float32)


def contract_k(x, weights, block_k):
    rows, depth = x.shape
    steps = depth // block_k
    out_bytes = sum(rows * w.shape[1] * 4 for w in weights)
    w_bytes = sum(w.size * w.dtype.itemsize for w in weights)
    return pl.pallas_call(
        _contract_k_kernel,
        grid=(steps,),
        in_specs=[pl.BlockSpec((rows, block_k), lambda k: (0, k))]
        + [pl.BlockSpec((block_k, w.shape[1]), lambda k: (k, 0)) for w in weights],
        out_specs=[pl.BlockSpec((rows, w.shape[1]), lambda k: (0, 0)) for w in weights],
        out_shape=[jax.ShapeDtypeStruct((rows, w.shape[1]), jnp.float32) for w in weights],
        compiler_params=pltpu.CompilerParams(dimension_semantics=("arbitrary",)),
        cost_estimate=pl.CostEstimate(
            flops=2 * rows * depth * sum(w.shape[1] for w in weights),
            bytes_accessed=w_bytes + x.size * x.dtype.itemsize + out_bytes,
            transcendentals=0,
        ),
    )(x, *weights)


def _contract_n_kernel(x_ref, w_ref, o_ref):
    o_ref[...] = jnp.dot(x_ref[...], w_ref[...], preferred_element_type=jnp.float32)


def contract_n(x, weight, block_n):
    rows, depth = x.shape
    width = weight.shape[1]
    steps = width // block_n
    return pl.pallas_call(
        _contract_n_kernel,
        grid=(steps,),
        in_specs=[
            pl.BlockSpec((rows, depth), lambda j: (0, 0)),
            pl.BlockSpec((depth, block_n), lambda j: (0, j)),
        ],
        out_specs=pl.BlockSpec((rows, block_n), lambda j: (0, j)),
        out_shape=jax.ShapeDtypeStruct((rows, width), jnp.float32),
        compiler_params=pltpu.CompilerParams(dimension_semantics=("arbitrary",)),
        cost_estimate=pl.CostEstimate(
            flops=2 * rows * depth * width,
            bytes_accessed=weight.size * weight.dtype.itemsize + x.size * 2 + rows * width * 4,
            transcendentals=0,
        ),
    )(x, weight)


def pick_block(size, target):
    block = target
    while size % block:
        block //= 2
    return block


def tensor_allreduce(part, tp_count):
    step = 1
    while step < tp_count:
        pairs = [(i, i ^ step) for i in range(tp_count)]
        part = part + lax.ppermute(part, "tensor", pairs)
        step *= 2
    return part


def local(
    residual_in,
    norm_gain,
    w_query,
    key_weight,
    value_weight,
    key_page_pool,
    value_page_pool,
    lengths,
    page_table,
    w_output,
    mlp_gain,
    w_gate,
    w_up,
    w_down,
):
    dp_count = lax.axis_size("dp")
    tp_count = lax.axis_size("tensor")
    rows_loc = residual_in.shape[0]
    req_loc = rows_loc * tp_count
    kv_loc = key_page_pool.shape[1]
    q_loc = w_query.shape[1] // HEAD_SIZE
    group_width = q_loc // kv_loc
    pool_size = key_page_pool.shape[0]
    page_len = key_page_pool.shape[3]
    per_req = page_table.shape[1]
    total_reqs = page_table.shape[0]
    score_scale = 1.0 / HEAD_SIZE**0.5
    dp_index = lax.axis_index("dp")
    tp_index = lax.axis_index("tensor")

    rows_all = lax.all_to_all(
        jnp.tile(residual_in, (dp_count * tp_count, 1)),
        ("dp", "tensor"),
        0,
        0,
        tiled=True,
    )

    request_ids = jnp.arange(total_reqs, dtype=jnp.int32)
    ranking = lengths * total_reqs + request_ids
    rank = jnp.sum((ranking[None, :] < ranking[:, None]).astype(jnp.int32), axis=1)
    round_no = rank // dp_count
    column = rank % dp_count
    server = jnp.where(round_no % 2 == 0, column, dp_count - 1 - column)
    slots = jnp.arange(req_loc, dtype=jnp.int32)
    hits = (server[None, :] == dp_index) & (round_no[None, :] == slots[:, None])
    served = jnp.sum(jnp.where(hits, request_ids[None, :], 0), axis=1)
    served_len = lengths[served]

    rows_srv = rows_all[served]
    scaled_input = norm_rows(rows_srv, norm_gain).astype(jnp.bfloat16)
    block_k = pick_block(scaled_input.shape[1], 512)
    q_acc, k_acc, v_acc = contract_k(scaled_input, [w_query, key_weight, value_weight], block_k)
    query_srv = (
        apply_rotation(q_acc.reshape(req_loc, q_loc, HEAD_SIZE), served_len)
        .astype(jnp.bfloat16)
        .reshape(req_loc, kv_loc, group_width, HEAD_SIZE)
    )
    key_srv = apply_rotation(k_acc.reshape(req_loc, kv_loc, HEAD_SIZE), served_len).astype(
        jnp.bfloat16
    )
    value_srv = v_acc.astype(jnp.bfloat16).reshape(req_loc, kv_loc, HEAD_SIZE)

    page_list = page_table[served] - dp_index * pool_size
    key_rows = key_page_pool[page_list]
    value_rows = value_page_pool[page_list]
    scores = (
        jnp.einsum("rhgd,rphdc->rhgpc", query_srv, key_rows, preferred_element_type=jnp.float32)
        * score_scale
    )
    positions = (
        jnp.arange(per_req, dtype=jnp.int32)[:, None] * page_len
        + jnp.arange(page_len, dtype=jnp.int32)[None, :]
    )
    valid_pos = (positions[None, :, :] < served_len[:, None, None])[:, None, None, :, :]
    own_score = (
        jnp.einsum("rhgd,rhd->rhg", query_srv, key_srv, preferred_element_type=jnp.float32)
        * score_scale
    )
    best = jnp.maximum(jnp.max(jnp.where(valid_pos, scores, -1e30), axis=(-2, -1)), own_score)
    weights = jnp.where(valid_pos, jnp.exp(scores - best[..., None, None]), 0.0)
    own_weight = jnp.exp(own_score - best)
    numer = (
        jnp.einsum("rhgpc,rphdc->rhgd", weights, value_rows.astype(jnp.float32))
        + own_weight[..., None] * value_srv.astype(jnp.float32)[:, :, None, :]
    )
    denom = jnp.sum(weights, axis=(-2, -1)) + own_weight
    attended = (numer / denom[..., None]).reshape(req_loc, q_loc * HEAD_SIZE).astype(jnp.bfloat16)

    summed = tensor_allreduce(
        jnp.dot(attended, w_output, preferred_element_type=jnp.float32), tp_count
    )
    mixed = rows_srv.astype(jnp.float32) + summed
    normed_mlp = norm_rows(mixed, mlp_gain).astype(jnp.bfloat16)
    gate_act, up_act = contract_k(normed_mlp, [w_gate, w_up], block_k)
    hidden = (jax.nn.silu(gate_act) * up_act).astype(jnp.bfloat16)
    down_sum = tensor_allreduce(
        contract_n(hidden, w_down, pick_block(w_down.shape[1], 512)), tp_count
    )
    final = (mixed + down_sum).astype(jnp.bfloat16)

    dest_rows = (
        jnp.arange(dp_count, dtype=jnp.int32)[:, None] * req_loc
        + tp_index * rows_loc
        + jnp.arange(rows_loc, dtype=jnp.int32)[None, :]
    ).reshape(-1)
    outgoing = final[round_no[dest_rows]]
    incoming = lax.all_to_all(outgoing, "dp", 0, 0, tiled=True)
    mine = dp_index * req_loc + tp_index * rows_loc + jnp.arange(rows_loc, dtype=jnp.int32)
    pick = server[mine] * rows_loc + jnp.arange(rows_loc, dtype=jnp.int32)
    return incoming[pick]


def solution(mesh):
    return jax.shard_map(
        local,
        mesh=mesh,
        in_specs=(
            P(("dp", "tensor"), None),
            P(),
            P(None, "tensor"),
            P(None, "tensor"),
            P(None, "tensor"),
            P("dp", "tensor", None, None),
            P("dp", "tensor", None, None),
            P(),
            P(),
            P("tensor", None),
            P(),
            P(None, "tensor"),
            P(None, "tensor"),
            P("tensor", None),
        ),
        out_specs=P(("dp", "tensor"), None),
        check_vma=False,
    )
```

```python
import jax
import jax.numpy as jnp
from jax import lax
from jax.sharding import PartitionSpec as P

HEAD_SIZE = 80


def norm_rows(value_rows, gain):
    value_rows = value_rows.astype(jnp.float32)
    return (
        value_rows
        * lax.rsqrt(jnp.mean(value_rows * value_rows, axis=-1, keepdims=True) + 1e-05)
        * gain.astype(jnp.float32)
    )


def apply_rotation(tensor, positions):
    half_dim = tensor.shape[-1] // 2
    inverse_freq = 1000000.0 ** (
        -(jnp.arange(half_dim, dtype=jnp.float32) * 2.0 / tensor.shape[-1])
    )
    angles = positions.astype(jnp.float32)[:, None] * inverse_freq[None, :]
    cosine = jnp.cos(angles)[:, None, :]
    sines = jnp.sin(angles)[:, None, :]
    first_half = tensor[..., :half_dim]
    second_half = tensor[..., half_dim:]
    return jnp.concatenate(
        [first_half * cosine - second_half * sines, second_half * cosine + first_half * sines],
        axis=-1,
    )


def tensor_allreduce(part, tp_count):
    step = 1
    while step < tp_count:
        pairs = [(i, i ^ step) for i in range(tp_count)]
        part = part + lax.ppermute(part, "tensor", pairs)
        step *= 2
    return part


def local(
    residual_in,
    norm_gain,
    w_query,
    key_weight,
    value_weight,
    key_page_pool,
    value_page_pool,
    lengths,
    page_table,
    w_output,
    mlp_gain,
    w_gate,
    w_up,
    w_down,
):
    dp_count = lax.axis_size("dp")
    tp_count = lax.axis_size("tensor")
    rows_loc = residual_in.shape[0]
    req_loc = rows_loc * tp_count
    kv_loc = key_page_pool.shape[1]
    q_loc = w_query.shape[1] // HEAD_SIZE
    group_width = q_loc // kv_loc
    pool_size = key_page_pool.shape[0]
    page_len = key_page_pool.shape[3]
    per_req = page_table.shape[1]
    total_reqs = page_table.shape[0]
    score_scale = 1.0 / HEAD_SIZE**0.5
    dp_index = lax.axis_index("dp")
    tp_index = lax.axis_index("tensor")

    dev_count = dp_count * tp_count
    rows_all = lax.all_to_all(
        jnp.broadcast_to(residual_in[None], (dev_count,) + residual_in.shape),
        ("dp", "tensor"),
        0,
        0,
    )

    request_ids = jnp.arange(total_reqs, dtype=jnp.int32)
    ranking = lengths * total_reqs + request_ids
    rank = jnp.sum((ranking[None, :] < ranking[:, None]).astype(jnp.int32), axis=1)
    round_no = rank // dp_count
    column = rank % dp_count
    server = jnp.where(round_no % 2 == 0, column, dp_count - 1 - column)
    slots = jnp.arange(req_loc, dtype=jnp.int32)
    hits = (server[None, :] == dp_index) & (round_no[None, :] == slots[:, None])
    served = jnp.sum(jnp.where(hits, request_ids[None, :], 0), axis=1)
    served_len = lengths[served]

    rows_srv = rows_all[served // rows_loc, served % rows_loc]
    scaled_input = norm_rows(rows_srv, norm_gain).astype(jnp.bfloat16)
    query_srv = (
        apply_rotation(
            jnp.dot(scaled_input, w_query, preferred_element_type=jnp.float32).reshape(
                req_loc, q_loc, HEAD_SIZE
            ),
            served_len,
        )
        .astype(jnp.bfloat16)
        .reshape(req_loc, kv_loc, group_width, HEAD_SIZE)
    )
    key_srv = apply_rotation(
        jnp.dot(scaled_input, key_weight, preferred_element_type=jnp.float32).reshape(
            req_loc, kv_loc, HEAD_SIZE
        ),
        served_len,
    ).astype(jnp.bfloat16)
    value_srv = (
        jnp.dot(scaled_input, value_weight, preferred_element_type=jnp.float32)
        .astype(jnp.bfloat16)
        .reshape(req_loc, kv_loc, HEAD_SIZE)
    )

    page_list = page_table[served] - dp_index * pool_size
    key_rows = key_page_pool[page_list]
    value_rows = value_page_pool[page_list]
    scores = (
        jnp.einsum("rhgd,rphdc->rhgpc", query_srv, key_rows, preferred_element_type=jnp.float32)
        * score_scale
    )
    positions = (
        jnp.arange(per_req, dtype=jnp.int32)[:, None] * page_len
        + jnp.arange(page_len, dtype=jnp.int32)[None, :]
    )
    valid_pos = (positions[None, :, :] < served_len[:, None, None])[:, None, None, :, :]
    own_score = (
        jnp.einsum("rhgd,rhd->rhg", query_srv, key_srv, preferred_element_type=jnp.float32)
        * score_scale
    )
    best = jnp.maximum(jnp.max(jnp.where(valid_pos, scores, -1e30), axis=(-2, -1)), own_score)
    weights = jnp.where(valid_pos, jnp.exp(scores - best[..., None, None]), 0.0)
    own_weight = jnp.exp(own_score - best)
    numer = (
        jnp.einsum("rhgpc,rphdc->rhgd", weights, value_rows.astype(jnp.float32))
        + own_weight[..., None] * value_srv.astype(jnp.float32)[:, :, None, :]
    )
    denom = jnp.sum(weights, axis=(-2, -1)) + own_weight
    attended = (numer / denom[..., None]).reshape(req_loc, q_loc * HEAD_SIZE).astype(jnp.bfloat16)

    summed = tensor_allreduce(
        jnp.dot(attended, w_output, preferred_element_type=jnp.float32), tp_count
    )
    mixed = rows_srv.astype(jnp.float32) + summed
    normed_mlp = norm_rows(mixed, mlp_gain).astype(jnp.bfloat16)
    gate_act = jnp.dot(normed_mlp, w_gate, preferred_element_type=jnp.float32)
    up_act = jnp.dot(normed_mlp, w_up, preferred_element_type=jnp.float32)
    hidden = (jax.nn.silu(gate_act) * up_act).astype(jnp.bfloat16)
    down_sum = tensor_allreduce(
        jnp.dot(hidden, w_down, preferred_element_type=jnp.float32), tp_count
    )
    final = (mixed + down_sum).astype(jnp.bfloat16)

    dest_rows = (
        jnp.arange(dp_count, dtype=jnp.int32)[:, None] * req_loc
        + tp_index * rows_loc
        + jnp.arange(rows_loc, dtype=jnp.int32)[None, :]
    ).reshape(-1)
    outgoing = final[round_no[dest_rows]].reshape(dp_count, rows_loc, final.shape[1])
    incoming = lax.all_to_all(outgoing, "dp", 0, 0)
    mine = dp_index * req_loc + tp_index * rows_loc + jnp.arange(rows_loc, dtype=jnp.int32)
    return incoming[server[mine], jnp.arange(rows_loc, dtype=jnp.int32)]


def solution(mesh):
    return jax.shard_map(
        local,
        mesh=mesh,
        in_specs=(
            P(("dp", "tensor"), None),
            P(),
            P(None, "tensor"),
            P(None, "tensor"),
            P(None, "tensor"),
            P("dp", "tensor", None, None),
            P("dp", "tensor", None, None),
            P(),
            P(),
            P("tensor", None),
            P(),
            P(None, "tensor"),
            P(None, "tensor"),
            P("tensor", None),
        ),
        out_specs=P(("dp", "tensor"), None),
        check_vma=False,
    )
```

```python
import jax
import jax.numpy as jnp
from jax import lax
from jax.sharding import PartitionSpec as P

HEAD_SIZE = 80


def norm_rows(value_rows, gain):
    value_rows = value_rows.astype(jnp.float32)
    return (
        value_rows
        * lax.rsqrt(jnp.mean(value_rows * value_rows, axis=-1, keepdims=True) + 1e-05)
        * gain.astype(jnp.float32)
    )


def apply_rotation(tensor, positions):
    half_dim = tensor.shape[-1] // 2
    inverse_freq = 1000000.0 ** (
        -(jnp.arange(half_dim, dtype=jnp.float32) * 2.0 / tensor.shape[-1])
    )
    angles = positions.astype(jnp.float32)[:, None] * inverse_freq[None, :]
    cosine = jnp.cos(angles)[:, None, :]
    sines = jnp.sin(angles)[:, None, :]
    first_half = tensor[..., :half_dim]
    second_half = tensor[..., half_dim:]
    return jnp.concatenate(
        [first_half * cosine - second_half * sines, second_half * cosine + first_half * sines],
        axis=-1,
    )


def tensor_allreduce(part, tp_count):
    step = 1
    while step < tp_count:
        pairs = [(i, i ^ step) for i in range(tp_count)]
        part = part + lax.ppermute(part, "tensor", pairs)
        step *= 2
    return part


def local(
    residual_in,
    norm_gain,
    w_query,
    key_weight,
    value_weight,
    key_page_pool,
    value_page_pool,
    lengths,
    page_table,
    w_output,
    mlp_gain,
    w_gate,
    w_up,
    w_down,
):
    dp_count = lax.axis_size("dp")
    tp_count = lax.axis_size("tensor")
    rows_loc = residual_in.shape[0]
    req_loc = rows_loc * tp_count
    kv_loc = key_page_pool.shape[1]
    q_loc = w_query.shape[1] // HEAD_SIZE
    group_width = q_loc // kv_loc
    pool_size = key_page_pool.shape[0]
    page_len = key_page_pool.shape[3]
    per_req = page_table.shape[1]
    total_reqs = page_table.shape[0]
    score_scale = 1.0 / HEAD_SIZE**0.5
    dp_index = lax.axis_index("dp")
    tp_index = lax.axis_index("tensor")

    dev_count = dp_count * tp_count
    rows_all = lax.all_to_all(
        jnp.broadcast_to(residual_in[None], (dev_count,) + residual_in.shape),
        ("dp", "tensor"),
        0,
        0,
    )

    request_ids = jnp.arange(total_reqs, dtype=jnp.int32)
    ranking = lengths * total_reqs + request_ids
    rank = jnp.sum((ranking[None, :] < ranking[:, None]).astype(jnp.int32), axis=1)
    round_no = rank // dp_count
    column = rank % dp_count
    server = jnp.where(round_no % 2 == 0, column, dp_count - 1 - column)
    slots = jnp.arange(req_loc, dtype=jnp.int32)
    hits = (server[None, :] == dp_index) & (round_no[None, :] == slots[:, None])
    served = jnp.sum(jnp.where(hits, request_ids[None, :], 0), axis=1)
    served_len = lengths[served]

    rows_srv = rows_all[served // rows_loc, served % rows_loc]
    scaled_input = norm_rows(rows_srv, norm_gain).astype(jnp.bfloat16)
    query_srv = (
        apply_rotation(
            jnp.dot(scaled_input, w_query, preferred_element_type=jnp.float32).reshape(
                req_loc, q_loc, HEAD_SIZE
            ),
            served_len,
        )
        .astype(jnp.bfloat16)
        .reshape(req_loc, kv_loc, group_width, HEAD_SIZE)
    )
    key_srv = apply_rotation(
        jnp.dot(scaled_input, key_weight, preferred_element_type=jnp.float32).reshape(
            req_loc, kv_loc, HEAD_SIZE
        ),
        served_len,
    ).astype(jnp.bfloat16)
    value_srv = (
        jnp.dot(scaled_input, value_weight, preferred_element_type=jnp.float32)
        .astype(jnp.bfloat16)
        .reshape(req_loc, kv_loc, HEAD_SIZE)
    )

    page_list = page_table[served] - dp_index * pool_size
    key_rows = key_page_pool[page_list]
    value_rows = value_page_pool[page_list]
    scores = (
        jnp.einsum("rhgd,rphdc->rhgpc", query_srv, key_rows, preferred_element_type=jnp.float32)
        * score_scale
    )
    positions = (
        jnp.arange(per_req, dtype=jnp.int32)[:, None] * page_len
        + jnp.arange(page_len, dtype=jnp.int32)[None, :]
    )
    valid_pos = (positions[None, :, :] < served_len[:, None, None])[:, None, None, :, :]
    own_score = (
        jnp.einsum("rhgd,rhd->rhg", query_srv, key_srv, preferred_element_type=jnp.float32)
        * score_scale
    )
    best = jnp.maximum(jnp.max(jnp.where(valid_pos, scores, -1e30), axis=(-2, -1)), own_score)
    weights = jnp.where(valid_pos, jnp.exp(scores - best[..., None, None]), 0.0)
    own_weight = jnp.exp(own_score - best)
    numer = (
        jnp.einsum("rhgpc,rphdc->rhgd", weights, value_rows.astype(jnp.float32))
        + own_weight[..., None] * value_srv.astype(jnp.float32)[:, :, None, :]
    )
    denom = jnp.sum(weights, axis=(-2, -1)) + own_weight
    attended = (numer / denom[..., None]).reshape(req_loc, q_loc * HEAD_SIZE).astype(jnp.bfloat16)

    summed = tensor_allreduce(
        jnp.dot(attended, w_output, preferred_element_type=jnp.float32), tp_count
    )
    mixed = rows_srv.astype(jnp.float32) + summed
    normed_mlp = norm_rows(mixed, mlp_gain).astype(jnp.bfloat16)
    gate_act = jnp.dot(normed_mlp, w_gate, preferred_element_type=jnp.float32)
    up_act = jnp.dot(normed_mlp, w_up, preferred_element_type=jnp.float32)
    hidden = (jax.nn.silu(gate_act) * up_act).astype(jnp.bfloat16)
    down_sum = tensor_allreduce(
        jnp.dot(hidden, w_down, preferred_element_type=jnp.float32), tp_count
    )
    final = (mixed + down_sum).astype(jnp.bfloat16)

    dest_rows = (
        jnp.arange(dp_count, dtype=jnp.int32)[:, None] * req_loc
        + tp_index * rows_loc
        + jnp.arange(rows_loc, dtype=jnp.int32)[None, :]
    ).reshape(-1)
    outgoing = final[round_no[dest_rows].reshape(dp_count, rows_loc)]
    incoming = lax.all_to_all(outgoing, "dp", 0, 0)
    mine = dp_index * req_loc + tp_index * rows_loc + jnp.arange(rows_loc, dtype=jnp.int32)
    from_src = jnp.arange(dp_count, dtype=jnp.int32)[:, None] == server[mine][None, :]
    picked = jnp.where(from_src[:, :, None], incoming.astype(jnp.float32), 0.0)
    return jnp.sum(picked, axis=0).astype(jnp.bfloat16)


def solution(mesh):
    return jax.shard_map(
        local,
        mesh=mesh,
        in_specs=(
            P(("dp", "tensor"), None),
            P(),
            P(None, "tensor"),
            P(None, "tensor"),
            P(None, "tensor"),
            P("dp", "tensor", None, None),
            P("dp", "tensor", None, None),
            P(),
            P(),
            P("tensor", None),
            P(),
            P(None, "tensor"),
            P(None, "tensor"),
            P("tensor", None),
        ),
        out_specs=P(("dp", "tensor"), None),
        check_vma=False,
    )
```

```python
import jax
import jax.numpy as jnp
from jax import lax
from jax.sharding import PartitionSpec as P

HEAD_SIZE = 80


def norm_rows(value_rows, gain):
    value_rows = value_rows.astype(jnp.float32)
    return (
        value_rows
        * lax.rsqrt(jnp.mean(value_rows * value_rows, axis=-1, keepdims=True) + 1e-05)
        * gain.astype(jnp.float32)
    )


def apply_rotation(tensor, positions):
    half_dim = tensor.shape[-1] // 2
    inverse_freq = 1000000.0 ** (
        -(jnp.arange(half_dim, dtype=jnp.float32) * 2.0 / tensor.shape[-1])
    )
    angles = positions.astype(jnp.float32)[:, None] * inverse_freq[None, :]
    cosine = jnp.cos(angles)[:, None, :]
    sines = jnp.sin(angles)[:, None, :]
    first_half = tensor[..., :half_dim]
    second_half = tensor[..., half_dim:]
    return jnp.concatenate(
        [first_half * cosine - second_half * sines, second_half * cosine + first_half * sines],
        axis=-1,
    )


def tensor_allreduce(part, tp_count):
    step = 1
    while step < tp_count:
        pairs = [(i, i ^ step) for i in range(tp_count)]
        part = part + lax.ppermute(part, "tensor", pairs)
        step *= 2
    return part


def local(
    residual_in,
    norm_gain,
    w_query,
    key_weight,
    value_weight,
    key_page_pool,
    value_page_pool,
    lengths,
    page_table,
    w_output,
    mlp_gain,
    w_gate,
    w_up,
    w_down,
):
    dp_count = lax.axis_size("dp")
    tp_count = lax.axis_size("tensor")
    rows_loc = residual_in.shape[0]
    req_loc = rows_loc * tp_count
    kv_loc = key_page_pool.shape[1]
    q_loc = w_query.shape[1] // HEAD_SIZE
    group_width = q_loc // kv_loc
    pool_size = key_page_pool.shape[0]
    page_len = key_page_pool.shape[3]
    per_req = page_table.shape[1]
    total_reqs = page_table.shape[0]
    score_scale = 1.0 / HEAD_SIZE**0.5
    dp_index = lax.axis_index("dp")
    tp_index = lax.axis_index("tensor")

    dev_count = dp_count * tp_count
    width = residual_in.shape[1]
    sub = 8
    packed = residual_in.reshape(rows_loc * sub, width // sub)
    rows_all = lax.all_to_all(
        jnp.broadcast_to(packed[None], (dev_count,) + packed.shape), ("dp", "tensor"), 0, 0
    )

    request_ids = jnp.arange(total_reqs, dtype=jnp.int32)
    ranking = lengths * total_reqs + request_ids
    rank = jnp.sum((ranking[None, :] < ranking[:, None]).astype(jnp.int32), axis=1)
    round_no = rank // dp_count
    column = rank % dp_count
    server = jnp.where(round_no % 2 == 0, column, dp_count - 1 - column)
    slots = jnp.arange(req_loc, dtype=jnp.int32)
    hits = (server[None, :] == dp_index) & (round_no[None, :] == slots[:, None])
    served = jnp.sum(jnp.where(hits, request_ids[None, :], 0), axis=1)
    served_len = lengths[served]

    sub_rows = (served % rows_loc)[:, None] * sub + jnp.arange(sub, dtype=jnp.int32)[None, :]
    rows_srv = rows_all[(served // rows_loc)[:, None], sub_rows].reshape(req_loc, width)
    rows_srv = lax.optimization_barrier(rows_srv)
    scaled_input = norm_rows(rows_srv, norm_gain).astype(jnp.bfloat16)
    query_srv = (
        apply_rotation(
            jnp.dot(scaled_input, w_query, preferred_element_type=jnp.float32).reshape(
                req_loc, q_loc, HEAD_SIZE
            ),
            served_len,
        )
        .astype(jnp.bfloat16)
        .reshape(req_loc, kv_loc, group_width, HEAD_SIZE)
    )
    key_srv = apply_rotation(
        jnp.dot(scaled_input, key_weight, preferred_element_type=jnp.float32).reshape(
            req_loc, kv_loc, HEAD_SIZE
        ),
        served_len,
    ).astype(jnp.bfloat16)
    value_srv = (
        jnp.dot(scaled_input, value_weight, preferred_element_type=jnp.float32)
        .astype(jnp.bfloat16)
        .reshape(req_loc, kv_loc, HEAD_SIZE)
    )

    page_list = page_table[served] - dp_index * pool_size
    key_rows = key_page_pool[page_list]
    value_rows = value_page_pool[page_list]
    scores = (
        jnp.einsum("rhgd,rphdc->rhgpc", query_srv, key_rows, preferred_element_type=jnp.float32)
        * score_scale
    )
    positions = (
        jnp.arange(per_req, dtype=jnp.int32)[:, None] * page_len
        + jnp.arange(page_len, dtype=jnp.int32)[None, :]
    )
    valid_pos = (positions[None, :, :] < served_len[:, None, None])[:, None, None, :, :]
    own_score = (
        jnp.einsum("rhgd,rhd->rhg", query_srv, key_srv, preferred_element_type=jnp.float32)
        * score_scale
    )
    best = jnp.maximum(jnp.max(jnp.where(valid_pos, scores, -1e30), axis=(-2, -1)), own_score)
    weights = jnp.where(valid_pos, jnp.exp(scores - best[..., None, None]), 0.0)
    own_weight = jnp.exp(own_score - best)
    numer = (
        jnp.einsum("rhgpc,rphdc->rhgd", weights, value_rows.astype(jnp.float32))
        + own_weight[..., None] * value_srv.astype(jnp.float32)[:, :, None, :]
    )
    denom = jnp.sum(weights, axis=(-2, -1)) + own_weight
    attended = (numer / denom[..., None]).reshape(req_loc, q_loc * HEAD_SIZE).astype(jnp.bfloat16)

    summed = tensor_allreduce(
        jnp.dot(attended, w_output, preferred_element_type=jnp.float32), tp_count
    )
    mixed = rows_srv.astype(jnp.float32) + summed
    normed_mlp = norm_rows(mixed, mlp_gain).astype(jnp.bfloat16)
    gate_act = jnp.dot(normed_mlp, w_gate, preferred_element_type=jnp.float32)
    up_act = jnp.dot(normed_mlp, w_up, preferred_element_type=jnp.float32)
    hidden = (jax.nn.silu(gate_act) * up_act).astype(jnp.bfloat16)
    down_sum = tensor_allreduce(
        jnp.dot(hidden, w_down, preferred_element_type=jnp.float32), tp_count
    )
    final = (mixed + down_sum).astype(jnp.bfloat16)

    dest_rows = (
        jnp.arange(dp_count, dtype=jnp.int32)[:, None] * req_loc
        + tp_index * rows_loc
        + jnp.arange(rows_loc, dtype=jnp.int32)[None, :]
    ).reshape(-1)
    outgoing = final[round_no[dest_rows].reshape(dp_count, rows_loc)]
    incoming = lax.all_to_all(outgoing, "dp", 0, 0)
    mine = dp_index * req_loc + tp_index * rows_loc + jnp.arange(rows_loc, dtype=jnp.int32)
    from_src = jnp.arange(dp_count, dtype=jnp.int32)[:, None] == server[mine][None, :]
    picked = jnp.where(from_src[:, :, None], incoming.astype(jnp.float32), 0.0)
    return jnp.sum(picked, axis=0).astype(jnp.bfloat16)


def solution(mesh):
    return jax.shard_map(
        local,
        mesh=mesh,
        in_specs=(
            P(("dp", "tensor"), None),
            P(),
            P(None, "tensor"),
            P(None, "tensor"),
            P(None, "tensor"),
            P("dp", "tensor", None, None),
            P("dp", "tensor", None, None),
            P(),
            P(),
            P("tensor", None),
            P(),
            P(None, "tensor"),
            P(None, "tensor"),
            P("tensor", None),
        ),
        out_specs=P(("dp", "tensor"), None),
        check_vma=False,
    )
```

```python
import jax
import jax.numpy as jnp
from jax import lax
from jax.sharding import PartitionSpec as P

HEAD_SIZE = 80


def norm_rows(value_rows, gain):
    value_rows = value_rows.astype(jnp.float32)
    return (
        value_rows
        * lax.rsqrt(jnp.mean(value_rows * value_rows, axis=-1, keepdims=True) + 1e-05)
        * gain.astype(jnp.float32)
    )


def apply_rotation(tensor, positions):
    half_dim = tensor.shape[-1] // 2
    inverse_freq = 1000000.0 ** (
        -(jnp.arange(half_dim, dtype=jnp.float32) * 2.0 / tensor.shape[-1])
    )
    angles = positions.astype(jnp.float32)[:, None] * inverse_freq[None, :]
    cosine = jnp.cos(angles)[:, None, :]
    sines = jnp.sin(angles)[:, None, :]
    first_half = tensor[..., :half_dim]
    second_half = tensor[..., half_dim:]
    return jnp.concatenate(
        [first_half * cosine - second_half * sines, second_half * cosine + first_half * sines],
        axis=-1,
    )


def tensor_allreduce(part, tp_count):
    step = 1
    while step < tp_count:
        pairs = [(i, i ^ step) for i in range(tp_count)]
        part = part + lax.ppermute(part, "tensor", pairs)
        step *= 2
    return part


def local(
    residual_in,
    norm_gain,
    w_query,
    key_weight,
    value_weight,
    key_page_pool,
    value_page_pool,
    lengths,
    page_table,
    w_output,
    mlp_gain,
    w_gate,
    w_up,
    w_down,
):
    dp_count = lax.axis_size("dp")
    tp_count = lax.axis_size("tensor")
    rows_loc = residual_in.shape[0]
    req_loc = rows_loc * tp_count
    kv_loc = key_page_pool.shape[1]
    q_loc = w_query.shape[1] // HEAD_SIZE
    group_width = q_loc // kv_loc
    pool_size = key_page_pool.shape[0]
    page_len = key_page_pool.shape[3]
    per_req = page_table.shape[1]
    total_reqs = page_table.shape[0]
    score_scale = 1.0 / HEAD_SIZE**0.5
    dp_index = lax.axis_index("dp")
    tp_index = lax.axis_index("tensor")

    dev_count = dp_count * tp_count
    rows_all = lax.all_to_all(
        jnp.broadcast_to(residual_in[None], (dev_count,) + residual_in.shape),
        ("dp", "tensor"),
        0,
        0,
    )

    request_ids = jnp.arange(total_reqs, dtype=jnp.int32)
    ranking = lengths * total_reqs + request_ids
    rank = jnp.sum((ranking[None, :] < ranking[:, None]).astype(jnp.int32), axis=1)
    round_no = rank // dp_count
    column = rank % dp_count
    server = jnp.where(round_no % 2 == 0, column, dp_count - 1 - column)
    slots = jnp.arange(req_loc, dtype=jnp.int32)
    hits = (server[None, :] == dp_index) & (round_no[None, :] == slots[:, None])
    served = jnp.sum(jnp.where(hits, request_ids[None, :], 0), axis=1)
    served_len = jnp.sum(jnp.where(hits, lengths[None, :], 0), axis=1)
    served_pages = jnp.sum(jnp.where(hits[:, :, None], page_table[None, :, :], 0), axis=1)

    rows_srv = rows_all[served // rows_loc, served % rows_loc]
    scaled_input = norm_rows(rows_srv, norm_gain).astype(jnp.bfloat16)
    query_srv = (
        apply_rotation(
            jnp.dot(scaled_input, w_query, preferred_element_type=jnp.float32).reshape(
                req_loc, q_loc, HEAD_SIZE
            ),
            served_len,
        )
        .astype(jnp.bfloat16)
        .reshape(req_loc, kv_loc, group_width, HEAD_SIZE)
    )
    key_srv = apply_rotation(
        jnp.dot(scaled_input, key_weight, preferred_element_type=jnp.float32).reshape(
            req_loc, kv_loc, HEAD_SIZE
        ),
        served_len,
    ).astype(jnp.bfloat16)
    value_srv = (
        jnp.dot(scaled_input, value_weight, preferred_element_type=jnp.float32)
        .astype(jnp.bfloat16)
        .reshape(req_loc, kv_loc, HEAD_SIZE)
    )

    page_list = (served_pages - dp_index * pool_size).reshape(-1)
    page_hot = (
        page_list[:, None] == jnp.arange(pool_size, dtype=jnp.int32)[None, :]
    ).astype(key_page_pool.dtype)
    key_rows = jnp.einsum(
        "sq,qhdc->shdc", page_hot, key_page_pool, preferred_element_type=jnp.bfloat16
    ).reshape((req_loc, per_req) + key_page_pool.shape[1:])
    value_rows = jnp.einsum(
        "sq,qhdc->shdc", page_hot, value_page_pool, preferred_element_type=jnp.bfloat16
    ).reshape((req_loc, per_req) + value_page_pool.shape[1:])
    scores = (
        jnp.einsum("rhgd,rphdc->rhgpc", query_srv, key_rows, preferred_element_type=jnp.float32)
        * score_scale
    )
    positions = (
        jnp.arange(per_req, dtype=jnp.int32)[:, None] * page_len
        + jnp.arange(page_len, dtype=jnp.int32)[None, :]
    )
    valid_pos = (positions[None, :, :] < served_len[:, None, None])[:, None, None, :, :]
    own_score = (
        jnp.einsum("rhgd,rhd->rhg", query_srv, key_srv, preferred_element_type=jnp.float32)
        * score_scale
    )
    best = jnp.maximum(jnp.max(jnp.where(valid_pos, scores, -1e30), axis=(-2, -1)), own_score)
    weights = jnp.where(valid_pos, jnp.exp(scores - best[..., None, None]), 0.0)
    own_weight = jnp.exp(own_score - best)
    numer = (
        jnp.einsum("rhgpc,rphdc->rhgd", weights, value_rows.astype(jnp.float32))
        + own_weight[..., None] * value_srv.astype(jnp.float32)[:, :, None, :]
    )
    denom = jnp.sum(weights, axis=(-2, -1)) + own_weight
    attended = (numer / denom[..., None]).reshape(req_loc, q_loc * HEAD_SIZE).astype(jnp.bfloat16)

    summed = tensor_allreduce(
        jnp.dot(attended, w_output, preferred_element_type=jnp.float32), tp_count
    )
    mixed = rows_srv.astype(jnp.float32) + summed
    normed_mlp = norm_rows(mixed, mlp_gain).astype(jnp.bfloat16)
    gate_act = jnp.dot(normed_mlp, w_gate, preferred_element_type=jnp.float32)
    up_act = jnp.dot(normed_mlp, w_up, preferred_element_type=jnp.float32)
    hidden = (jax.nn.silu(gate_act) * up_act).astype(jnp.bfloat16)
    down_sum = tensor_allreduce(
        jnp.dot(hidden, w_down, preferred_element_type=jnp.float32), tp_count
    )
    final = (mixed + down_sum).astype(jnp.bfloat16)

    dest_rows = (
        jnp.arange(dp_count, dtype=jnp.int32)[:, None] * req_loc
        + tp_index * rows_loc
        + jnp.arange(rows_loc, dtype=jnp.int32)[None, :]
    ).reshape(-1)
    dest_round = jnp.sum(
        jnp.where(request_ids[None, :] == dest_rows[:, None], round_no[None, :], 0), axis=1
    )
    outgoing = final[dest_round.reshape(dp_count, rows_loc)]
    incoming = lax.all_to_all(outgoing, "dp", 0, 0)
    mine = dp_index * req_loc + tp_index * rows_loc + jnp.arange(rows_loc, dtype=jnp.int32)
    from_src = jnp.arange(dp_count, dtype=jnp.int32)[:, None] == server[mine][None, :]
    picked = jnp.where(from_src[:, :, None], incoming.astype(jnp.float32), 0.0)
    return jnp.sum(picked, axis=0).astype(jnp.bfloat16)


def solution(mesh):
    return jax.shard_map(
        local,
        mesh=mesh,
        in_specs=(
            P(("dp", "tensor"), None),
            P(),
            P(None, "tensor"),
            P(None, "tensor"),
            P(None, "tensor"),
            P("dp", "tensor", None, None),
            P("dp", "tensor", None, None),
            P(),
            P(),
            P("tensor", None),
            P(),
            P(None, "tensor"),
            P(None, "tensor"),
            P("tensor", None),
        ),
        out_specs=P(("dp", "tensor"), None),
        check_vma=False,
    )
```

```python
import jax
import jax.numpy as jnp
from jax import lax
from jax.sharding import PartitionSpec as P

HEAD_SIZE = 80


def norm_rows(value_rows, gain):
    value_rows = value_rows.astype(jnp.float32)
    return (
        value_rows
        * lax.rsqrt(jnp.mean(value_rows * value_rows, axis=-1, keepdims=True) + 1e-05)
        * gain.astype(jnp.float32)
    )


def apply_rotation(tensor, positions):
    half_dim = tensor.shape[-1] // 2
    inverse_freq = 1000000.0 ** (
        -(jnp.arange(half_dim, dtype=jnp.float32) * 2.0 / tensor.shape[-1])
    )
    angles = positions.astype(jnp.float32)[:, None] * inverse_freq[None, :]
    cosine = jnp.cos(angles)[:, None, :]
    sines = jnp.sin(angles)[:, None, :]
    first_half = tensor[..., :half_dim]
    second_half = tensor[..., half_dim:]
    return jnp.concatenate(
        [first_half * cosine - second_half * sines, second_half * cosine + first_half * sines],
        axis=-1,
    )


def tensor_allreduce(part, tp_count):
    step = 1
    while step < tp_count:
        pairs = [(i, i ^ step) for i in range(tp_count)]
        part = part + lax.ppermute(part, "tensor", pairs)
        step *= 2
    return part


def local(
    residual_in,
    norm_gain,
    w_query,
    key_weight,
    value_weight,
    key_page_pool,
    value_page_pool,
    lengths,
    page_table,
    w_output,
    mlp_gain,
    w_gate,
    w_up,
    w_down,
):
    dp_count = lax.axis_size("dp")
    tp_count = lax.axis_size("tensor")
    rows_loc = residual_in.shape[0]
    req_loc = rows_loc * tp_count
    kv_loc = key_page_pool.shape[1]
    q_loc = w_query.shape[1] // HEAD_SIZE
    group_width = q_loc // kv_loc
    pool_size = key_page_pool.shape[0]
    page_len = key_page_pool.shape[3]
    per_req = page_table.shape[1]
    total_reqs = page_table.shape[0]
    score_scale = 1.0 / HEAD_SIZE**0.5
    dp_index = lax.axis_index("dp")
    tp_index = lax.axis_index("tensor")

    dev_count = dp_count * tp_count
    rows_all = lax.all_to_all(
        jnp.broadcast_to(residual_in[None], (dev_count,) + residual_in.shape),
        ("dp", "tensor"),
        0,
        0,
    )

    request_ids = jnp.arange(total_reqs, dtype=jnp.int32)
    ranking = lengths * total_reqs + request_ids
    rank = jnp.sum((ranking[None, :] < ranking[:, None]).astype(jnp.int32), axis=1)
    round_no = rank // dp_count
    column = rank % dp_count
    server = jnp.where(round_no % 2 == 0, column, dp_count - 1 - column)
    slots = jnp.arange(req_loc, dtype=jnp.int32)
    hits = (server[None, :] == dp_index) & (round_no[None, :] == slots[:, None])
    served = jnp.sum(jnp.where(hits, request_ids[None, :], 0), axis=1)
    served_len = jnp.sum(jnp.where(hits, lengths[None, :], 0), axis=1)
    served_pages = jnp.sum(jnp.where(hits[:, :, None], page_table[None, :, :], 0), axis=1)

    rows_srv = rows_all[served // rows_loc, served % rows_loc]
    scaled_input = norm_rows(rows_srv, norm_gain).astype(jnp.bfloat16)
    query_srv = (
        apply_rotation(
            jnp.dot(scaled_input, w_query, preferred_element_type=jnp.float32).reshape(
                req_loc, q_loc, HEAD_SIZE
            ),
            served_len,
        )
        .astype(jnp.bfloat16)
        .reshape(req_loc, kv_loc, group_width, HEAD_SIZE)
    )
    key_srv = apply_rotation(
        jnp.dot(scaled_input, key_weight, preferred_element_type=jnp.float32).reshape(
            req_loc, kv_loc, HEAD_SIZE
        ),
        served_len,
    ).astype(jnp.bfloat16)
    value_srv = (
        jnp.dot(scaled_input, value_weight, preferred_element_type=jnp.float32)
        .astype(jnp.bfloat16)
        .reshape(req_loc, kv_loc, HEAD_SIZE)
    )

    page_list = (served_pages - dp_index * pool_size).reshape(-1)
    page_hot = (
        page_list[:, None] == jnp.arange(pool_size, dtype=jnp.int32)[None, :]
    ).astype(key_page_pool.dtype)
    key_rows = jnp.einsum(
        "sq,qhdc->shdc", page_hot, key_page_pool, preferred_element_type=jnp.bfloat16
    ).reshape((req_loc, per_req) + key_page_pool.shape[1:])
    value_rows = jnp.einsum(
        "sq,qhdc->shdc", page_hot, value_page_pool, preferred_element_type=jnp.bfloat16
    ).reshape((req_loc, per_req) + value_page_pool.shape[1:])
    scores = (
        jnp.einsum("rhgd,rphdc->rhgpc", query_srv, key_rows, preferred_element_type=jnp.float32)
        * score_scale
    )
    positions = (
        jnp.arange(per_req, dtype=jnp.int32)[:, None] * page_len
        + jnp.arange(page_len, dtype=jnp.int32)[None, :]
    )
    valid_pos = (positions[None, :, :] < served_len[:, None, None])[:, None, None, :, :]
    own_score = (
        jnp.einsum("rhgd,rhd->rhg", query_srv, key_srv, preferred_element_type=jnp.float32)
        * score_scale
    )
    best = jnp.maximum(jnp.max(jnp.where(valid_pos, scores, -1e30), axis=(-2, -1)), own_score)
    weights = jnp.where(valid_pos, jnp.exp(scores - best[..., None, None]), 0.0)
    own_weight = jnp.exp(own_score - best)
    numer = (
        jnp.einsum("rhgpc,rphdc->rhgd", weights, value_rows.astype(jnp.float32))
        + own_weight[..., None] * value_srv.astype(jnp.float32)[:, :, None, :]
    )
    denom = jnp.sum(weights, axis=(-2, -1)) + own_weight
    attended = (numer / denom[..., None]).reshape(req_loc, q_loc * HEAD_SIZE).astype(jnp.bfloat16)

    summed = tensor_allreduce(
        jnp.dot(attended, w_output, preferred_element_type=jnp.float32), tp_count
    )
    mixed = rows_srv.astype(jnp.float32) + summed
    normed_mlp = norm_rows(mixed, mlp_gain).astype(jnp.bfloat16)
    gate_act = jnp.dot(normed_mlp, w_gate, preferred_element_type=jnp.float32)
    up_act = jnp.dot(normed_mlp, w_up, preferred_element_type=jnp.float32)
    hidden = (jax.nn.silu(gate_act) * up_act).astype(jnp.bfloat16)
    down_sum = tensor_allreduce(
        jnp.dot(hidden, w_down, preferred_element_type=jnp.float32), tp_count
    )
    final = (mixed + down_sum).astype(jnp.bfloat16)

    dest_rows = (
        jnp.arange(dp_count, dtype=jnp.int32)[:, None] * req_loc
        + tp_index * rows_loc
        + jnp.arange(rows_loc, dtype=jnp.int32)[None, :]
    ).reshape(-1)
    dest_round = jnp.sum(
        jnp.where(request_ids[None, :] == dest_rows[:, None], round_no[None, :], 0), axis=1
    )
    send_hot = dest_round.reshape(dp_count, rows_loc)[:, :, None] == slots[None, None, :]
    outgoing = jnp.sum(
        jnp.where(send_hot[:, :, :, None], final.astype(jnp.float32)[None, None], 0.0), axis=2
    ).astype(jnp.bfloat16)
    incoming = lax.all_to_all(outgoing, "dp", 0, 0)
    mine = dp_index * req_loc + tp_index * rows_loc + jnp.arange(rows_loc, dtype=jnp.int32)
    from_src = jnp.arange(dp_count, dtype=jnp.int32)[:, None] == server[mine][None, :]
    picked = jnp.where(from_src[:, :, None], incoming.astype(jnp.float32), 0.0)
    return jnp.sum(picked, axis=0).astype(jnp.bfloat16)


def solution(mesh):
    return jax.shard_map(
        local,
        mesh=mesh,
        in_specs=(
            P(("dp", "tensor"), None),
            P(),
            P(None, "tensor"),
            P(None, "tensor"),
            P(None, "tensor"),
            P("dp", "tensor", None, None),
            P("dp", "tensor", None, None),
            P(),
            P(),
            P("tensor", None),
            P(),
            P(None, "tensor"),
            P(None, "tensor"),
            P("tensor", None),
        ),
        out_specs=P(("dp", "tensor"), None),
        check_vma=False,
    )
```

```python
import jax
import jax.numpy as jnp
from jax import lax
from jax.sharding import PartitionSpec as P

HEAD_SIZE = 80


def norm_rows(value_rows, gain):
    value_rows = value_rows.astype(jnp.float32)
    return (
        value_rows
        * lax.rsqrt(jnp.mean(value_rows * value_rows, axis=-1, keepdims=True) + 1e-05)
        * gain.astype(jnp.float32)
    )


def apply_rotation(tensor, positions):
    half_dim = tensor.shape[-1] // 2
    inverse_freq = 1000000.0 ** (
        -(jnp.arange(half_dim, dtype=jnp.float32) * 2.0 / tensor.shape[-1])
    )
    angles = positions.astype(jnp.float32)[:, None] * inverse_freq[None, :]
    cosine = jnp.cos(angles)[:, None, :]
    sines = jnp.sin(angles)[:, None, :]
    first_half = tensor[..., :half_dim]
    second_half = tensor[..., half_dim:]
    return jnp.concatenate(
        [first_half * cosine - second_half * sines, second_half * cosine + first_half * sines],
        axis=-1,
    )


def tensor_allreduce(part, tp_count):
    def shifted(value, k):
        return lax.ppermute(value, "tensor", [(i, (i + k) % tp_count) for i in range(tp_count)])

    if tp_count == 4:
        return (part + shifted(part, 2)) + (shifted(part, 1) + shifted(part, 3))
    step = 1
    while step < tp_count:
        part = part + lax.ppermute(part, "tensor", [(i, i ^ step) for i in range(tp_count)])
        step *= 2
    return part


def local(
    residual_in,
    norm_gain,
    w_query,
    key_weight,
    value_weight,
    key_page_pool,
    value_page_pool,
    lengths,
    page_table,
    w_output,
    mlp_gain,
    w_gate,
    w_up,
    w_down,
):
    dp_count = lax.axis_size("dp")
    tp_count = lax.axis_size("tensor")
    rows_loc = residual_in.shape[0]
    req_loc = rows_loc * tp_count
    kv_loc = key_page_pool.shape[1]
    q_loc = w_query.shape[1] // HEAD_SIZE
    group_width = q_loc // kv_loc
    pool_size = key_page_pool.shape[0]
    page_len = key_page_pool.shape[3]
    per_req = page_table.shape[1]
    total_reqs = page_table.shape[0]
    score_scale = 1.0 / HEAD_SIZE**0.5
    dp_index = lax.axis_index("dp")
    tp_index = lax.axis_index("tensor")

    dev_count = dp_count * tp_count
    rows_all = lax.all_to_all(
        jnp.broadcast_to(residual_in[None], (dev_count,) + residual_in.shape),
        ("dp", "tensor"),
        0,
        0,
    )

    request_ids = jnp.arange(total_reqs, dtype=jnp.int32)
    ranking = lengths * total_reqs + request_ids
    rank = jnp.sum((ranking[None, :] < ranking[:, None]).astype(jnp.int32), axis=1)
    round_no = rank // dp_count
    column = rank % dp_count
    server = jnp.where(round_no % 2 == 0, column, dp_count - 1 - column)
    slots = jnp.arange(req_loc, dtype=jnp.int32)
    hits = (server[None, :] == dp_index) & (round_no[None, :] == slots[:, None])
    served = jnp.sum(jnp.where(hits, request_ids[None, :], 0), axis=1)
    served_len = jnp.sum(jnp.where(hits, lengths[None, :], 0), axis=1)
    served_pages = jnp.sum(jnp.where(hits[:, :, None], page_table[None, :, :], 0), axis=1)

    rows_srv = rows_all[served // rows_loc, served % rows_loc]
    scaled_input = norm_rows(rows_srv, norm_gain).astype(jnp.bfloat16)
    query_srv = (
        apply_rotation(
            jnp.dot(scaled_input, w_query, preferred_element_type=jnp.float32).reshape(
                req_loc, q_loc, HEAD_SIZE
            ),
            served_len,
        )
        .astype(jnp.bfloat16)
        .reshape(req_loc, kv_loc, group_width, HEAD_SIZE)
    )
    key_srv = apply_rotation(
        jnp.dot(scaled_input, key_weight, preferred_element_type=jnp.float32).reshape(
            req_loc, kv_loc, HEAD_SIZE
        ),
        served_len,
    ).astype(jnp.bfloat16)
    value_srv = (
        jnp.dot(scaled_input, value_weight, preferred_element_type=jnp.float32)
        .astype(jnp.bfloat16)
        .reshape(req_loc, kv_loc, HEAD_SIZE)
    )

    page_list = (served_pages - dp_index * pool_size).reshape(-1)
    page_hot = (
        page_list[:, None] == jnp.arange(pool_size, dtype=jnp.int32)[None, :]
    ).astype(key_page_pool.dtype)
    key_rows = jnp.einsum(
        "sq,qhdc->shdc", page_hot, key_page_pool, preferred_element_type=jnp.bfloat16
    ).reshape((req_loc, per_req) + key_page_pool.shape[1:])
    value_rows = jnp.einsum(
        "sq,qhdc->shdc", page_hot, value_page_pool, preferred_element_type=jnp.bfloat16
    ).reshape((req_loc, per_req) + value_page_pool.shape[1:])
    scores = (
        jnp.einsum("rhgd,rphdc->rhgpc", query_srv, key_rows, preferred_element_type=jnp.float32)
        * score_scale
    )
    positions = (
        jnp.arange(per_req, dtype=jnp.int32)[:, None] * page_len
        + jnp.arange(page_len, dtype=jnp.int32)[None, :]
    )
    valid_pos = (positions[None, :, :] < served_len[:, None, None])[:, None, None, :, :]
    own_score = (
        jnp.einsum("rhgd,rhd->rhg", query_srv, key_srv, preferred_element_type=jnp.float32)
        * score_scale
    )
    best = jnp.maximum(jnp.max(jnp.where(valid_pos, scores, -1e30), axis=(-2, -1)), own_score)
    weights = jnp.where(valid_pos, jnp.exp(scores - best[..., None, None]), 0.0)
    own_weight = jnp.exp(own_score - best)
    numer = (
        jnp.einsum("rhgpc,rphdc->rhgd", weights, value_rows.astype(jnp.float32))
        + own_weight[..., None] * value_srv.astype(jnp.float32)[:, :, None, :]
    )
    denom = jnp.sum(weights, axis=(-2, -1)) + own_weight
    attended = (numer / denom[..., None]).reshape(req_loc, q_loc * HEAD_SIZE).astype(jnp.bfloat16)

    summed = tensor_allreduce(
        jnp.dot(attended, w_output, preferred_element_type=jnp.float32), tp_count
    )
    mixed = rows_srv.astype(jnp.float32) + summed
    normed_mlp = norm_rows(mixed, mlp_gain).astype(jnp.bfloat16)
    gate_act = jnp.dot(normed_mlp, w_gate, preferred_element_type=jnp.float32)
    up_act = jnp.dot(normed_mlp, w_up, preferred_element_type=jnp.float32)
    hidden = (jax.nn.silu(gate_act) * up_act).astype(jnp.bfloat16)
    down_sum = tensor_allreduce(
        jnp.dot(hidden, w_down, preferred_element_type=jnp.float32), tp_count
    )
    final = (mixed + down_sum).astype(jnp.bfloat16)

    dest_rows = (
        jnp.arange(dp_count, dtype=jnp.int32)[:, None] * req_loc
        + tp_index * rows_loc
        + jnp.arange(rows_loc, dtype=jnp.int32)[None, :]
    ).reshape(-1)
    dest_round = jnp.sum(
        jnp.where(request_ids[None, :] == dest_rows[:, None], round_no[None, :], 0), axis=1
    )
    outgoing = final[dest_round.reshape(dp_count, rows_loc)]
    incoming = lax.all_to_all(outgoing, "dp", 0, 0)
    mine = dp_index * req_loc + tp_index * rows_loc + jnp.arange(rows_loc, dtype=jnp.int32)
    from_src = jnp.arange(dp_count, dtype=jnp.int32)[:, None] == server[mine][None, :]
    picked = jnp.where(from_src[:, :, None], incoming.astype(jnp.float32), 0.0)
    return jnp.sum(picked, axis=0).astype(jnp.bfloat16)


def solution(mesh):
    return jax.shard_map(
        local,
        mesh=mesh,
        in_specs=(
            P(("dp", "tensor"), None),
            P(),
            P(None, "tensor"),
            P(None, "tensor"),
            P(None, "tensor"),
            P("dp", "tensor", None, None),
            P("dp", "tensor", None, None),
            P(),
            P(),
            P("tensor", None),
            P(),
            P(None, "tensor"),
            P(None, "tensor"),
            P("tensor", None),
        ),
        out_specs=P(("dp", "tensor"), None),
        check_vma=False,
    )
```

```python
import jax
import jax.numpy as jnp
from jax import lax
from jax.sharding import PartitionSpec as P

HEAD_SIZE = 80


def norm_rows(value_rows, gain):
    value_rows = value_rows.astype(jnp.float32)
    return (
        value_rows
        * lax.rsqrt(jnp.mean(value_rows * value_rows, axis=-1, keepdims=True) + 1e-05)
        * gain.astype(jnp.float32)
    )


def apply_rotation(tensor, positions):
    half_dim = tensor.shape[-1] // 2
    inverse_freq = 1000000.0 ** (
        -(jnp.arange(half_dim, dtype=jnp.float32) * 2.0 / tensor.shape[-1])
    )
    angles = positions.astype(jnp.float32)[:, None] * inverse_freq[None, :]
    cosine = jnp.cos(angles)[:, None, :]
    sines = jnp.sin(angles)[:, None, :]
    first_half = tensor[..., :half_dim]
    second_half = tensor[..., half_dim:]
    return jnp.concatenate(
        [first_half * cosine - second_half * sines, second_half * cosine + first_half * sines],
        axis=-1,
    )


def tensor_allreduce(part, tp_count):
    def shifted(value, k):
        return lax.ppermute(value, "tensor", [(i, (i + k) % tp_count) for i in range(tp_count)])

    if tp_count == 4:
        return (part + shifted(part, 2)) + (shifted(part, 1) + shifted(part, 3))
    step = 1
    while step < tp_count:
        part = part + lax.ppermute(part, "tensor", [(i, i ^ step) for i in range(tp_count)])
        step *= 2
    return part


def local(
    residual_in,
    norm_gain,
    w_query,
    key_weight,
    value_weight,
    key_page_pool,
    value_page_pool,
    lengths,
    page_table,
    w_output,
    mlp_gain,
    w_gate,
    w_up,
    w_down,
):
    dp_count = lax.axis_size("dp")
    tp_count = lax.axis_size("tensor")
    rows_loc = residual_in.shape[0]
    req_loc = rows_loc * tp_count
    kv_loc = key_page_pool.shape[1]
    q_loc = w_query.shape[1] // HEAD_SIZE
    group_width = q_loc // kv_loc
    pool_size = key_page_pool.shape[0]
    page_len = key_page_pool.shape[3]
    per_req = page_table.shape[1]
    total_reqs = page_table.shape[0]
    score_scale = 1.0 / HEAD_SIZE**0.5
    dp_index = lax.axis_index("dp")
    tp_index = lax.axis_index("tensor")

    dev_count = dp_count * tp_count
    rows_all = lax.all_to_all(
        jnp.broadcast_to(residual_in[None], (dev_count,) + residual_in.shape),
        ("dp", "tensor"),
        0,
        0,
    )

    request_ids = jnp.arange(total_reqs, dtype=jnp.int32)
    ranking = lengths * total_reqs + request_ids
    rank = jnp.sum((ranking[None, :] < ranking[:, None]).astype(jnp.int32), axis=1)
    round_no = rank // dp_count
    column = rank % dp_count
    server = jnp.where(round_no % 2 == 0, column, dp_count - 1 - column)
    slots = jnp.arange(req_loc, dtype=jnp.int32)
    hits = (server[None, :] == dp_index) & (round_no[None, :] == slots[:, None])
    served = jnp.sum(jnp.where(hits, request_ids[None, :], 0), axis=1)
    served_len = jnp.sum(jnp.where(hits, lengths[None, :], 0), axis=1)
    served_pages = jnp.sum(jnp.where(hits[:, :, None], page_table[None, :, :], 0), axis=1)

    width = residual_in.shape[1]
    rows_srv = jnp.concatenate(
        [
            lax.dynamic_slice(
                rows_all, (served[i] // rows_loc, served[i] % rows_loc, 0), (1, 1, width)
            ).reshape(1, width)
            for i in range(req_loc)
        ],
        axis=0,
    )
    scaled_input = norm_rows(rows_srv, norm_gain).astype(jnp.bfloat16)
    query_srv = (
        apply_rotation(
            jnp.dot(scaled_input, w_query, preferred_element_type=jnp.float32).reshape(
                req_loc, q_loc, HEAD_SIZE
            ),
            served_len,
        )
        .astype(jnp.bfloat16)
        .reshape(req_loc, kv_loc, group_width, HEAD_SIZE)
    )
    key_srv = apply_rotation(
        jnp.dot(scaled_input, key_weight, preferred_element_type=jnp.float32).reshape(
            req_loc, kv_loc, HEAD_SIZE
        ),
        served_len,
    ).astype(jnp.bfloat16)
    value_srv = (
        jnp.dot(scaled_input, value_weight, preferred_element_type=jnp.float32)
        .astype(jnp.bfloat16)
        .reshape(req_loc, kv_loc, HEAD_SIZE)
    )

    page_list = (served_pages - dp_index * pool_size).reshape(-1)
    page_hot = (
        page_list[:, None] == jnp.arange(pool_size, dtype=jnp.int32)[None, :]
    ).astype(key_page_pool.dtype)
    key_rows = jnp.einsum(
        "sq,qhdc->shdc", page_hot, key_page_pool, preferred_element_type=jnp.bfloat16
    ).reshape((req_loc, per_req) + key_page_pool.shape[1:])
    value_rows = jnp.einsum(
        "sq,qhdc->shdc", page_hot, value_page_pool, preferred_element_type=jnp.bfloat16
    ).reshape((req_loc, per_req) + value_page_pool.shape[1:])
    scores = (
        jnp.einsum("rhgd,rphdc->rhgpc", query_srv, key_rows, preferred_element_type=jnp.float32)
        * score_scale
    )
    positions = (
        jnp.arange(per_req, dtype=jnp.int32)[:, None] * page_len
        + jnp.arange(page_len, dtype=jnp.int32)[None, :]
    )
    valid_pos = (positions[None, :, :] < served_len[:, None, None])[:, None, None, :, :]
    own_score = (
        jnp.einsum("rhgd,rhd->rhg", query_srv, key_srv, preferred_element_type=jnp.float32)
        * score_scale
    )
    best = jnp.maximum(jnp.max(jnp.where(valid_pos, scores, -1e30), axis=(-2, -1)), own_score)
    weights = jnp.where(valid_pos, jnp.exp(scores - best[..., None, None]), 0.0)
    own_weight = jnp.exp(own_score - best)
    numer = (
        jnp.einsum("rhgpc,rphdc->rhgd", weights, value_rows.astype(jnp.float32))
        + own_weight[..., None] * value_srv.astype(jnp.float32)[:, :, None, :]
    )
    denom = jnp.sum(weights, axis=(-2, -1)) + own_weight
    attended = (numer / denom[..., None]).reshape(req_loc, q_loc * HEAD_SIZE).astype(jnp.bfloat16)

    summed = tensor_allreduce(
        jnp.dot(attended, w_output, preferred_element_type=jnp.float32), tp_count
    )
    mixed = rows_srv.astype(jnp.float32) + summed
    normed_mlp = norm_rows(mixed, mlp_gain).astype(jnp.bfloat16)
    gate_act = jnp.dot(normed_mlp, w_gate, preferred_element_type=jnp.float32)
    up_act = jnp.dot(normed_mlp, w_up, preferred_element_type=jnp.float32)
    hidden = (jax.nn.silu(gate_act) * up_act).astype(jnp.bfloat16)
    down_sum = tensor_allreduce(
        jnp.dot(hidden, w_down, preferred_element_type=jnp.float32), tp_count
    )
    final = (mixed + down_sum).astype(jnp.bfloat16)

    dest_rows = (
        jnp.arange(dp_count, dtype=jnp.int32)[:, None] * req_loc
        + tp_index * rows_loc
        + jnp.arange(rows_loc, dtype=jnp.int32)[None, :]
    ).reshape(-1)
    dest_round = jnp.sum(
        jnp.where(request_ids[None, :] == dest_rows[:, None], round_no[None, :], 0), axis=1
    )
    outgoing = jnp.stack(
        [
            jnp.concatenate(
                [
                    lax.dynamic_slice(final, (dest_round[d * rows_loc + j], 0), (1, width))
                    for j in range(rows_loc)
                ],
                axis=0,
            )
            for d in range(dp_count)
        ]
    )
    incoming = lax.all_to_all(outgoing, "dp", 0, 0)
    mine = dp_index * req_loc + tp_index * rows_loc + jnp.arange(rows_loc, dtype=jnp.int32)
    from_src = jnp.arange(dp_count, dtype=jnp.int32)[:, None] == server[mine][None, :]
    picked = jnp.where(from_src[:, :, None], incoming.astype(jnp.float32), 0.0)
    return jnp.sum(picked, axis=0).astype(jnp.bfloat16)


def solution(mesh):
    return jax.shard_map(
        local,
        mesh=mesh,
        in_specs=(
            P(("dp", "tensor"), None),
            P(),
            P(None, "tensor"),
            P(None, "tensor"),
            P(None, "tensor"),
            P("dp", "tensor", None, None),
            P("dp", "tensor", None, None),
            P(),
            P(),
            P("tensor", None),
            P(),
            P(None, "tensor"),
            P(None, "tensor"),
            P("tensor", None),
        ),
        out_specs=P(("dp", "tensor"), None),
        check_vma=False,
    )
```

```python
import jax
import jax.numpy as jnp
from jax import lax
from jax.sharding import PartitionSpec as P

HEAD_SIZE = 80


def norm_rows(value_rows, gain):
    value_rows = value_rows.astype(jnp.float32)
    return (
        value_rows
        * lax.rsqrt(jnp.mean(value_rows * value_rows, axis=-1, keepdims=True) + 1e-05)
        * gain.astype(jnp.float32)
    )


def apply_rotation(tensor, positions):
    half_dim = tensor.shape[-1] // 2
    inverse_freq = 1000000.0 ** (
        -(jnp.arange(half_dim, dtype=jnp.float32) * 2.0 / tensor.shape[-1])
    )
    angles = positions.astype(jnp.float32)[:, None] * inverse_freq[None, :]
    cosine = jnp.cos(angles)[:, None, :]
    sines = jnp.sin(angles)[:, None, :]
    first_half = tensor[..., :half_dim]
    second_half = tensor[..., half_dim:]
    return jnp.concatenate(
        [first_half * cosine - second_half * sines, second_half * cosine + first_half * sines],
        axis=-1,
    )


def tensor_allreduce(part, tp_count):
    def shifted(value, k):
        return lax.ppermute(value, "tensor", [(i, (i + k) % tp_count) for i in range(tp_count)])

    if tp_count == 4:
        return (part + shifted(part, 2)) + (shifted(part, 1) + shifted(part, 3))
    step = 1
    while step < tp_count:
        part = part + lax.ppermute(part, "tensor", [(i, i ^ step) for i in range(tp_count)])
        step *= 2
    return part


def local(
    residual_in,
    norm_gain,
    w_query,
    key_weight,
    value_weight,
    key_page_pool,
    value_page_pool,
    lengths,
    page_table,
    w_output,
    mlp_gain,
    w_gate,
    w_up,
    w_down,
):
    dp_count = lax.axis_size("dp")
    tp_count = lax.axis_size("tensor")
    rows_loc = residual_in.shape[0]
    req_loc = rows_loc * tp_count
    kv_loc = key_page_pool.shape[1]
    q_loc = w_query.shape[1] // HEAD_SIZE
    group_width = q_loc // kv_loc
    pool_size = key_page_pool.shape[0]
    page_len = key_page_pool.shape[3]
    per_req = page_table.shape[1]
    total_reqs = page_table.shape[0]
    score_scale = 1.0 / HEAD_SIZE**0.5
    dp_index = lax.axis_index("dp")
    tp_index = lax.axis_index("tensor")

    rows_dp = lax.all_to_all(
        jnp.broadcast_to(residual_in[None], (dp_count,) + residual_in.shape), "dp", 0, 0
    )

    request_ids = jnp.arange(total_reqs, dtype=jnp.int32)
    ranking = lengths * total_reqs + request_ids
    rank = jnp.sum((ranking[None, :] < ranking[:, None]).astype(jnp.int32), axis=1)
    round_no = rank // dp_count
    column = rank % dp_count
    server = jnp.where(round_no % 2 == 0, column, dp_count - 1 - column)
    slots = jnp.arange(req_loc, dtype=jnp.int32)
    hits = (server[None, :] == dp_index) & (round_no[None, :] == slots[:, None])
    served = jnp.sum(jnp.where(hits, request_ids[None, :], 0), axis=1)
    served_len = jnp.sum(jnp.where(hits, lengths[None, :], 0), axis=1)
    served_pages = jnp.sum(jnp.where(hits[:, :, None], page_table[None, :, :], 0), axis=1)

    owner_tp = (served % req_loc) // rows_loc
    held = rows_dp[served // req_loc, served % rows_loc]
    held = jnp.where((owner_tp == tp_index)[:, None], held, jnp.zeros_like(held))
    rows_srv = tensor_allreduce(held, tp_count)
    scaled_input = norm_rows(rows_srv, norm_gain).astype(jnp.bfloat16)
    query_srv = (
        apply_rotation(
            jnp.dot(scaled_input, w_query, preferred_element_type=jnp.float32).reshape(
                req_loc, q_loc, HEAD_SIZE
            ),
            served_len,
        )
        .astype(jnp.bfloat16)
        .reshape(req_loc, kv_loc, group_width, HEAD_SIZE)
    )
    key_srv = apply_rotation(
        jnp.dot(scaled_input, key_weight, preferred_element_type=jnp.float32).reshape(
            req_loc, kv_loc, HEAD_SIZE
        ),
        served_len,
    ).astype(jnp.bfloat16)
    value_srv = (
        jnp.dot(scaled_input, value_weight, preferred_element_type=jnp.float32)
        .astype(jnp.bfloat16)
        .reshape(req_loc, kv_loc, HEAD_SIZE)
    )

    page_list = (served_pages - dp_index * pool_size).reshape(-1)
    page_hot = (
        page_list[:, None] == jnp.arange(pool_size, dtype=jnp.int32)[None, :]
    ).astype(key_page_pool.dtype)
    key_rows = jnp.einsum(
        "sq,qhdc->shdc", page_hot, key_page_pool, preferred_element_type=jnp.bfloat16
    ).reshape((req_loc, per_req) + key_page_pool.shape[1:])
    value_rows = jnp.einsum(
        "sq,qhdc->shdc", page_hot, value_page_pool, preferred_element_type=jnp.bfloat16
    ).reshape((req_loc, per_req) + value_page_pool.shape[1:])
    scores = (
        jnp.einsum("rhgd,rphdc->rhgpc", query_srv, key_rows, preferred_element_type=jnp.float32)
        * score_scale
    )
    positions = (
        jnp.arange(per_req, dtype=jnp.int32)[:, None] * page_len
        + jnp.arange(page_len, dtype=jnp.int32)[None, :]
    )
    valid_pos = (positions[None, :, :] < served_len[:, None, None])[:, None, None, :, :]
    own_score = (
        jnp.einsum("rhgd,rhd->rhg", query_srv, key_srv, preferred_element_type=jnp.float32)
        * score_scale
    )
    best = jnp.maximum(jnp.max(jnp.where(valid_pos, scores, -1e30), axis=(-2, -1)), own_score)
    weights = jnp.where(valid_pos, jnp.exp(scores - best[..., None, None]), 0.0)
    own_weight = jnp.exp(own_score - best)
    numer = (
        jnp.einsum("rhgpc,rphdc->rhgd", weights, value_rows.astype(jnp.float32))
        + own_weight[..., None] * value_srv.astype(jnp.float32)[:, :, None, :]
    )
    denom = jnp.sum(weights, axis=(-2, -1)) + own_weight
    attended = (numer / denom[..., None]).reshape(req_loc, q_loc * HEAD_SIZE).astype(jnp.bfloat16)

    summed = tensor_allreduce(
        jnp.dot(attended, w_output, preferred_element_type=jnp.float32), tp_count
    )
    mixed = rows_srv.astype(jnp.float32) + summed
    normed_mlp = norm_rows(mixed, mlp_gain).astype(jnp.bfloat16)
    gate_act = jnp.dot(normed_mlp, w_gate, preferred_element_type=jnp.float32)
    up_act = jnp.dot(normed_mlp, w_up, preferred_element_type=jnp.float32)
    hidden = (jax.nn.silu(gate_act) * up_act).astype(jnp.bfloat16)
    down_sum = tensor_allreduce(
        jnp.dot(hidden, w_down, preferred_element_type=jnp.float32), tp_count
    )
    final = (mixed + down_sum).astype(jnp.bfloat16)

    dest_rows = (
        jnp.arange(dp_count, dtype=jnp.int32)[:, None] * req_loc
        + tp_index * rows_loc
        + jnp.arange(rows_loc, dtype=jnp.int32)[None, :]
    ).reshape(-1)
    dest_round = jnp.sum(
        jnp.where(request_ids[None, :] == dest_rows[:, None], round_no[None, :], 0), axis=1
    )
    outgoing = final[dest_round.reshape(dp_count, rows_loc)]
    incoming = lax.all_to_all(outgoing, "dp", 0, 0)
    mine = dp_index * req_loc + tp_index * rows_loc + jnp.arange(rows_loc, dtype=jnp.int32)
    from_src = jnp.arange(dp_count, dtype=jnp.int32)[:, None] == server[mine][None, :]
    picked = jnp.where(from_src[:, :, None], incoming.astype(jnp.float32), 0.0)
    return jnp.sum(picked, axis=0).astype(jnp.bfloat16)


def solution(mesh):
    return jax.shard_map(
        local,
        mesh=mesh,
        in_specs=(
            P(("dp", "tensor"), None),
            P(),
            P(None, "tensor"),
            P(None, "tensor"),
            P(None, "tensor"),
            P("dp", "tensor", None, None),
            P("dp", "tensor", None, None),
            P(),
            P(),
            P("tensor", None),
            P(),
            P(None, "tensor"),
            P(None, "tensor"),
            P("tensor", None),
        ),
        out_specs=P(("dp", "tensor"), None),
        check_vma=False,
    )
```

```python
import jax
import jax.numpy as jnp
from jax import lax
from jax.sharding import PartitionSpec as P

HEAD_SIZE = 80


def norm_rows(value_rows, gain):
    value_rows = value_rows.astype(jnp.float32)
    return (
        value_rows
        * lax.rsqrt(jnp.mean(value_rows * value_rows, axis=-1, keepdims=True) + 1e-05)
        * gain.astype(jnp.float32)
    )


def apply_rotation(tensor, positions):
    half_dim = tensor.shape[-1] // 2
    inverse_freq = 1000000.0 ** (
        -(jnp.arange(half_dim, dtype=jnp.float32) * 2.0 / tensor.shape[-1])
    )
    angles = positions.astype(jnp.float32)[:, None] * inverse_freq[None, :]
    cosine = jnp.cos(angles)[:, None, :]
    sines = jnp.sin(angles)[:, None, :]
    first_half = tensor[..., :half_dim]
    second_half = tensor[..., half_dim:]
    return jnp.concatenate(
        [first_half * cosine - second_half * sines, second_half * cosine + first_half * sines],
        axis=-1,
    )


def tensor_allreduce(part, tp_count):
    def shifted(value, k):
        return lax.ppermute(value, "tensor", [(i, (i + k) % tp_count) for i in range(tp_count)])

    if tp_count == 4:
        return (part + shifted(part, 2)) + (shifted(part, 1) + shifted(part, 3))
    step = 1
    while step < tp_count:
        part = part + lax.ppermute(part, "tensor", [(i, i ^ step) for i in range(tp_count)])
        step *= 2
    return part


def local(
    residual_in,
    norm_gain,
    w_query,
    key_weight,
    value_weight,
    key_page_pool,
    value_page_pool,
    lengths,
    page_table,
    w_output,
    mlp_gain,
    w_gate,
    w_up,
    w_down,
):
    dp_count = lax.axis_size("dp")
    tp_count = lax.axis_size("tensor")
    rows_loc = residual_in.shape[0]
    req_loc = rows_loc * tp_count
    kv_loc = key_page_pool.shape[1]
    q_loc = w_query.shape[1] // HEAD_SIZE
    group_width = q_loc // kv_loc
    pool_size = key_page_pool.shape[0]
    page_len = key_page_pool.shape[3]
    per_req = page_table.shape[1]
    total_reqs = page_table.shape[0]
    score_scale = 1.0 / HEAD_SIZE**0.5
    dp_index = lax.axis_index("dp")
    tp_index = lax.axis_index("tensor")

    rows_dp = lax.all_to_all(
        jnp.broadcast_to(residual_in[None], (dp_count,) + residual_in.shape), "dp", 0, 0
    )

    request_ids = jnp.arange(total_reqs, dtype=jnp.int32)
    ranking = lengths * total_reqs + request_ids
    rank = jnp.sum((ranking[None, :] < ranking[:, None]).astype(jnp.int32), axis=1)
    round_no = rank // dp_count
    column = rank % dp_count
    server = jnp.where(round_no % 2 == 0, column, dp_count - 1 - column)
    slots = jnp.arange(req_loc, dtype=jnp.int32)
    hits = (server[None, :] == dp_index) & (round_no[None, :] == slots[:, None])
    served = jnp.sum(jnp.where(hits, request_ids[None, :], 0), axis=1)
    served_len = jnp.sum(jnp.where(hits, lengths[None, :], 0), axis=1)
    served_pages = jnp.sum(jnp.where(hits[:, :, None], page_table[None, :, :], 0), axis=1)

    owner_tp = (served % req_loc) // rows_loc
    held = rows_dp[served // req_loc, served % rows_loc]
    held = jnp.where((owner_tp == tp_index)[:, None], held, jnp.zeros_like(held))
    held, served_pages = lax.optimization_barrier((held, served_pages))
    rows_srv = tensor_allreduce(held, tp_count)
    scaled_input = norm_rows(rows_srv, norm_gain).astype(jnp.bfloat16)
    query_srv = (
        apply_rotation(
            jnp.dot(scaled_input, w_query, preferred_element_type=jnp.float32).reshape(
                req_loc, q_loc, HEAD_SIZE
            ),
            served_len,
        )
        .astype(jnp.bfloat16)
        .reshape(req_loc, kv_loc, group_width, HEAD_SIZE)
    )
    key_srv = apply_rotation(
        jnp.dot(scaled_input, key_weight, preferred_element_type=jnp.float32).reshape(
            req_loc, kv_loc, HEAD_SIZE
        ),
        served_len,
    ).astype(jnp.bfloat16)
    value_srv = (
        jnp.dot(scaled_input, value_weight, preferred_element_type=jnp.float32)
        .astype(jnp.bfloat16)
        .reshape(req_loc, kv_loc, HEAD_SIZE)
    )

    page_list = (served_pages - dp_index * pool_size).reshape(-1)
    page_hot = (
        page_list[:, None] == jnp.arange(pool_size, dtype=jnp.int32)[None, :]
    ).astype(key_page_pool.dtype)
    key_rows = jnp.einsum(
        "sq,qhdc->shdc", page_hot, key_page_pool, preferred_element_type=jnp.bfloat16
    ).reshape((req_loc, per_req) + key_page_pool.shape[1:])
    value_rows = jnp.einsum(
        "sq,qhdc->shdc", page_hot, value_page_pool, preferred_element_type=jnp.bfloat16
    ).reshape((req_loc, per_req) + value_page_pool.shape[1:])
    scores = (
        jnp.einsum("rhgd,rphdc->rhgpc", query_srv, key_rows, preferred_element_type=jnp.float32)
        * score_scale
    )
    positions = (
        jnp.arange(per_req, dtype=jnp.int32)[:, None] * page_len
        + jnp.arange(page_len, dtype=jnp.int32)[None, :]
    )
    valid_pos = (positions[None, :, :] < served_len[:, None, None])[:, None, None, :, :]
    own_score = (
        jnp.einsum("rhgd,rhd->rhg", query_srv, key_srv, preferred_element_type=jnp.float32)
        * score_scale
    )
    best = jnp.maximum(jnp.max(jnp.where(valid_pos, scores, -1e30), axis=(-2, -1)), own_score)
    weights = jnp.where(valid_pos, jnp.exp(scores - best[..., None, None]), 0.0)
    own_weight = jnp.exp(own_score - best)
    numer = (
        jnp.einsum("rhgpc,rphdc->rhgd", weights, value_rows.astype(jnp.float32))
        + own_weight[..., None] * value_srv.astype(jnp.float32)[:, :, None, :]
    )
    denom = jnp.sum(weights, axis=(-2, -1)) + own_weight
    attended = (numer / denom[..., None]).reshape(req_loc, q_loc * HEAD_SIZE).astype(jnp.bfloat16)

    summed = tensor_allreduce(
        jnp.dot(attended, w_output, preferred_element_type=jnp.float32), tp_count
    )
    mixed = rows_srv.astype(jnp.float32) + summed
    normed_mlp = norm_rows(mixed, mlp_gain).astype(jnp.bfloat16)
    gate_act = jnp.dot(normed_mlp, w_gate, preferred_element_type=jnp.float32)
    up_act = jnp.dot(normed_mlp, w_up, preferred_element_type=jnp.float32)
    hidden = (jax.nn.silu(gate_act) * up_act).astype(jnp.bfloat16)
    down_sum = tensor_allreduce(
        jnp.dot(hidden, w_down, preferred_element_type=jnp.float32), tp_count
    )
    final = (mixed + down_sum).astype(jnp.bfloat16)

    dest_rows = (
        jnp.arange(dp_count, dtype=jnp.int32)[:, None] * req_loc
        + tp_index * rows_loc
        + jnp.arange(rows_loc, dtype=jnp.int32)[None, :]
    ).reshape(-1)
    dest_round = jnp.sum(
        jnp.where(request_ids[None, :] == dest_rows[:, None], round_no[None, :], 0), axis=1
    )
    outgoing = final[dest_round.reshape(dp_count, rows_loc)]
    incoming = lax.all_to_all(outgoing, "dp", 0, 0)
    mine = dp_index * req_loc + tp_index * rows_loc + jnp.arange(rows_loc, dtype=jnp.int32)
    from_src = jnp.arange(dp_count, dtype=jnp.int32)[:, None] == server[mine][None, :]
    picked = jnp.where(from_src[:, :, None], incoming.astype(jnp.float32), 0.0)
    return jnp.sum(picked, axis=0).astype(jnp.bfloat16)


def solution(mesh):
    return jax.shard_map(
        local,
        mesh=mesh,
        in_specs=(
            P(("dp", "tensor"), None),
            P(),
            P(None, "tensor"),
            P(None, "tensor"),
            P(None, "tensor"),
            P("dp", "tensor", None, None),
            P("dp", "tensor", None, None),
            P(),
            P(),
            P("tensor", None),
            P(),
            P(None, "tensor"),
            P(None, "tensor"),
            P("tensor", None),
        ),
        out_specs=P(("dp", "tensor"), None),
        check_vma=False,
    )
```

```python
import jax
import jax.numpy as jnp
from jax import lax
from jax.sharding import PartitionSpec as P

HEAD_SIZE = 80


def norm_rows(value_rows, gain):
    value_rows = value_rows.astype(jnp.float32)
    return (
        value_rows
        * lax.rsqrt(jnp.mean(value_rows * value_rows, axis=-1, keepdims=True) + 1e-05)
        * gain.astype(jnp.float32)
    )


def apply_rotation(tensor, positions):
    half_dim = tensor.shape[-1] // 2
    inverse_freq = 1000000.0 ** (
        -(jnp.arange(half_dim, dtype=jnp.float32) * 2.0 / tensor.shape[-1])
    )
    angles = positions.astype(jnp.float32)[:, None] * inverse_freq[None, :]
    cosine = jnp.cos(angles)[:, None, :]
    sines = jnp.sin(angles)[:, None, :]
    first_half = tensor[..., :half_dim]
    second_half = tensor[..., half_dim:]
    return jnp.concatenate(
        [first_half * cosine - second_half * sines, second_half * cosine + first_half * sines],
        axis=-1,
    )


def tensor_allreduce(part, tp_count):
    def shifted(value, k):
        return lax.ppermute(value, "tensor", [(i, (i + k) % tp_count) for i in range(tp_count)])

    if tp_count == 4:
        return (part + shifted(part, 2)) + (shifted(part, 1) + shifted(part, 3))
    step = 1
    while step < tp_count:
        part = part + lax.ppermute(part, "tensor", [(i, i ^ step) for i in range(tp_count)])
        step *= 2
    return part


def local(
    residual_in,
    norm_gain,
    w_query,
    key_weight,
    value_weight,
    key_page_pool,
    value_page_pool,
    lengths,
    page_table,
    w_output,
    mlp_gain,
    w_gate,
    w_up,
    w_down,
):
    dp_count = lax.axis_size("dp")
    tp_count = lax.axis_size("tensor")
    rows_loc = residual_in.shape[0]
    req_loc = rows_loc * tp_count
    kv_loc = key_page_pool.shape[1]
    q_loc = w_query.shape[1] // HEAD_SIZE
    group_width = q_loc // kv_loc
    pool_size = key_page_pool.shape[0]
    page_len = key_page_pool.shape[3]
    per_req = page_table.shape[1]
    total_reqs = page_table.shape[0]
    score_scale = 1.0 / HEAD_SIZE**0.5
    dp_index = lax.axis_index("dp")
    tp_index = lax.axis_index("tensor")

    rows_dp = lax.all_to_all(
        jnp.broadcast_to(residual_in[None], (dp_count,) + residual_in.shape), "dp", 0, 0
    )

    request_ids = jnp.arange(total_reqs, dtype=jnp.int32)
    ranking = lengths * total_reqs + request_ids
    rank = jnp.sum((ranking[None, :] < ranking[:, None]).astype(jnp.int32), axis=1)
    round_no = rank // dp_count
    column = rank % dp_count
    server = jnp.where(round_no % 2 == 0, column, dp_count - 1 - column)
    slots = jnp.arange(req_loc, dtype=jnp.int32)
    hits = (server[None, :] == dp_index) & (round_no[None, :] == slots[:, None])
    served = jnp.sum(jnp.where(hits, request_ids[None, :], 0), axis=1)
    served_len = jnp.sum(jnp.where(hits, lengths[None, :], 0), axis=1)
    served_pages = jnp.sum(jnp.where(hits[:, :, None], page_table[None, :, :], 0), axis=1)

    owner_tp = (served % req_loc) // rows_loc
    held = rows_dp[served // req_loc, served % rows_loc]
    held = jnp.where((owner_tp == tp_index)[:, None], held, jnp.zeros_like(held))
    rows_srv = tensor_allreduce(held, tp_count)
    scaled_input = norm_rows(rows_srv, norm_gain).astype(jnp.bfloat16)
    query_srv = (
        apply_rotation(
            jnp.dot(scaled_input, w_query, preferred_element_type=jnp.float32).reshape(
                req_loc, q_loc, HEAD_SIZE
            ),
            served_len,
        )
        .astype(jnp.bfloat16)
        .reshape(req_loc, kv_loc, group_width, HEAD_SIZE)
    )
    key_srv = apply_rotation(
        jnp.dot(scaled_input, key_weight, preferred_element_type=jnp.float32).reshape(
            req_loc, kv_loc, HEAD_SIZE
        ),
        served_len,
    ).astype(jnp.bfloat16)
    value_srv = (
        jnp.dot(scaled_input, value_weight, preferred_element_type=jnp.float32)
        .astype(jnp.bfloat16)
        .reshape(req_loc, kv_loc, HEAD_SIZE)
    )

    page_loc = served_pages - dp_index * pool_size
    pool_ids = jnp.arange(pool_size, dtype=jnp.int32)
    match = page_loc[:, :, None] == pool_ids[None, None, :]
    page_start = jnp.arange(per_req, dtype=jnp.int32)[None, :, None] * page_len
    offset = jnp.where(
        jnp.any(match, axis=1),
        jnp.sum(jnp.where(match, page_start, 0), axis=1),
        per_req * page_len,
    )
    valid_pos = (
        offset[:, :, None] + jnp.arange(page_len, dtype=jnp.int32)[None, None, :]
        < served_len[:, None, None]
    )[:, None, None, :, :]
    scores = (
        jnp.einsum(
            "rhgd,qhdc->rhgqc", query_srv, key_page_pool, preferred_element_type=jnp.float32
        )
        * score_scale
    )
    own_score = (
        jnp.einsum("rhgd,rhd->rhg", query_srv, key_srv, preferred_element_type=jnp.float32)
        * score_scale
    )
    best = jnp.maximum(jnp.max(jnp.where(valid_pos, scores, -1e30), axis=(-2, -1)), own_score)
    weights = jnp.where(valid_pos, jnp.exp(scores - best[..., None, None]), 0.0)
    own_weight = jnp.exp(own_score - best)
    numer = (
        jnp.einsum("rhgqc,qhdc->rhgd", weights, value_page_pool.astype(jnp.float32))
        + own_weight[..., None] * value_srv.astype(jnp.float32)[:, :, None, :]
    )
    denom = jnp.sum(weights, axis=(-2, -1)) + own_weight
    attended = (numer / denom[..., None]).reshape(req_loc, q_loc * HEAD_SIZE).astype(jnp.bfloat16)

    summed = tensor_allreduce(
        jnp.dot(attended, w_output, preferred_element_type=jnp.float32), tp_count
    )
    mixed = rows_srv.astype(jnp.float32) + summed
    normed_mlp = norm_rows(mixed, mlp_gain).astype(jnp.bfloat16)
    gate_act = jnp.dot(normed_mlp, w_gate, preferred_element_type=jnp.float32)
    up_act = jnp.dot(normed_mlp, w_up, preferred_element_type=jnp.float32)
    hidden = (jax.nn.silu(gate_act) * up_act).astype(jnp.bfloat16)
    down_sum = tensor_allreduce(
        jnp.dot(hidden, w_down, preferred_element_type=jnp.float32), tp_count
    )
    final = (mixed + down_sum).astype(jnp.bfloat16)

    dest_rows = (
        jnp.arange(dp_count, dtype=jnp.int32)[:, None] * req_loc
        + tp_index * rows_loc
        + jnp.arange(rows_loc, dtype=jnp.int32)[None, :]
    ).reshape(-1)
    dest_round = jnp.sum(
        jnp.where(request_ids[None, :] == dest_rows[:, None], round_no[None, :], 0), axis=1
    )
    outgoing = final[dest_round.reshape(dp_count, rows_loc)]
    incoming = lax.all_to_all(outgoing, "dp", 0, 0)
    mine = dp_index * req_loc + tp_index * rows_loc + jnp.arange(rows_loc, dtype=jnp.int32)
    from_src = jnp.arange(dp_count, dtype=jnp.int32)[:, None] == server[mine][None, :]
    picked = jnp.where(from_src[:, :, None], incoming.astype(jnp.float32), 0.0)
    return jnp.sum(picked, axis=0).astype(jnp.bfloat16)


def solution(mesh):
    return jax.shard_map(
        local,
        mesh=mesh,
        in_specs=(
            P(("dp", "tensor"), None),
            P(),
            P(None, "tensor"),
            P(None, "tensor"),
            P(None, "tensor"),
            P("dp", "tensor", None, None),
            P("dp", "tensor", None, None),
            P(),
            P(),
            P("tensor", None),
            P(),
            P(None, "tensor"),
            P(None, "tensor"),
            P("tensor", None),
        ),
        out_specs=P(("dp", "tensor"), None),
        check_vma=False,
    )
```

```python
import jax
import jax.numpy as jnp
from jax import lax
from jax.sharding import PartitionSpec as P

HEAD_SIZE = 80


def norm_rows(value_rows, gain):
    value_rows = value_rows.astype(jnp.float32)
    return (
        value_rows
        * lax.rsqrt(jnp.mean(value_rows * value_rows, axis=-1, keepdims=True) + 1e-05)
        * gain.astype(jnp.float32)
    )


def apply_rotation(tensor, positions):
    half_dim = tensor.shape[-1] // 2
    inverse_freq = 1000000.0 ** (
        -(jnp.arange(half_dim, dtype=jnp.float32) * 2.0 / tensor.shape[-1])
    )
    angles = positions.astype(jnp.float32)[:, None] * inverse_freq[None, :]
    cosine = jnp.cos(angles)[:, None, :]
    sines = jnp.sin(angles)[:, None, :]
    first_half = tensor[..., :half_dim]
    second_half = tensor[..., half_dim:]
    return jnp.concatenate(
        [first_half * cosine - second_half * sines, second_half * cosine + first_half * sines],
        axis=-1,
    )


def tensor_allreduce(part, tp_count):
    def shifted(value, k):
        return lax.ppermute(value, "tensor", [(i, (i + k) % tp_count) for i in range(tp_count)])

    if tp_count == 4:
        return (part + shifted(part, 2)) + (shifted(part, 1) + shifted(part, 3))
    step = 1
    while step < tp_count:
        part = part + lax.ppermute(part, "tensor", [(i, i ^ step) for i in range(tp_count)])
        step *= 2
    return part


def local(
    residual_in,
    norm_gain,
    w_query,
    key_weight,
    value_weight,
    key_page_pool,
    value_page_pool,
    lengths,
    page_table,
    w_output,
    mlp_gain,
    w_gate,
    w_up,
    w_down,
):
    dp_count = lax.axis_size("dp")
    tp_count = lax.axis_size("tensor")
    rows_loc = residual_in.shape[0]
    req_loc = rows_loc * tp_count
    kv_loc = key_page_pool.shape[1]
    q_loc = w_query.shape[1] // HEAD_SIZE
    group_width = q_loc // kv_loc
    pool_size = key_page_pool.shape[0]
    page_len = key_page_pool.shape[3]
    per_req = page_table.shape[1]
    total_reqs = page_table.shape[0]
    score_scale = 1.0 / HEAD_SIZE**0.5
    dp_index = lax.axis_index("dp")
    tp_index = lax.axis_index("tensor")

    rows_dp = lax.all_to_all(
        jnp.broadcast_to(residual_in[None], (dp_count,) + residual_in.shape), "dp", 0, 0
    )

    request_ids = jnp.arange(total_reqs, dtype=jnp.int32)
    ranking = lengths * total_reqs + request_ids
    rank = jnp.sum((ranking[None, :] < ranking[:, None]).astype(jnp.int32), axis=1)
    round_no = rank // dp_count
    column = rank % dp_count
    server = jnp.where(round_no % 2 == 0, column, dp_count - 1 - column)
    slots = jnp.arange(req_loc, dtype=jnp.int32)
    hits = (server[None, :] == dp_index) & (round_no[None, :] == slots[:, None])
    served = jnp.sum(jnp.where(hits, request_ids[None, :], 0), axis=1)
    served_len = jnp.sum(jnp.where(hits, lengths[None, :], 0), axis=1)
    served_pages = jnp.sum(jnp.where(hits[:, :, None], page_table[None, :, :], 0), axis=1)

    owner_tp = (served % req_loc) // rows_loc
    held = rows_dp[served // req_loc, served % rows_loc]
    held = jnp.where((owner_tp == tp_index)[:, None], held, jnp.zeros_like(held))
    early_pages = served_pages
    held, served_pages = lax.optimization_barrier((held, served_pages))
    rows_srv = tensor_allreduce(held, tp_count)
    scaled_input = norm_rows(rows_srv, norm_gain).astype(jnp.bfloat16)
    query_srv = (
        apply_rotation(
            jnp.dot(scaled_input, w_query, preferred_element_type=jnp.float32).reshape(
                req_loc, q_loc, HEAD_SIZE
            ),
            served_len,
        )
        .astype(jnp.bfloat16)
        .reshape(req_loc, kv_loc, group_width, HEAD_SIZE)
    )
    key_srv = apply_rotation(
        jnp.dot(scaled_input, key_weight, preferred_element_type=jnp.float32).reshape(
            req_loc, kv_loc, HEAD_SIZE
        ),
        served_len,
    ).astype(jnp.bfloat16)
    value_srv = (
        jnp.dot(scaled_input, value_weight, preferred_element_type=jnp.float32)
        .astype(jnp.bfloat16)
        .reshape(req_loc, kv_loc, HEAD_SIZE)
    )

    page_list = (served_pages - dp_index * pool_size).reshape(-1)
    page_hot = (
        page_list[:, None] == jnp.arange(pool_size, dtype=jnp.int32)[None, :]
    ).astype(key_page_pool.dtype)
    key_rows = jnp.einsum(
        "sq,qhdc->shdc", page_hot, key_page_pool, preferred_element_type=jnp.bfloat16
    ).reshape((req_loc, per_req) + key_page_pool.shape[1:])
    early_hot = (
        (early_pages - dp_index * pool_size).reshape(-1)[:, None]
        == jnp.arange(pool_size, dtype=jnp.int32)[None, :]
    ).astype(value_page_pool.dtype)
    value_rows = jnp.einsum(
        "sq,qhdc->shdc", early_hot, value_page_pool, preferred_element_type=jnp.bfloat16
    ).reshape((req_loc, per_req) + value_page_pool.shape[1:])
    scores = (
        jnp.einsum("rhgd,rphdc->rhgpc", query_srv, key_rows, preferred_element_type=jnp.float32)
        * score_scale
    )
    positions = (
        jnp.arange(per_req, dtype=jnp.int32)[:, None] * page_len
        + jnp.arange(page_len, dtype=jnp.int32)[None, :]
    )
    valid_pos = (positions[None, :, :] < served_len[:, None, None])[:, None, None, :, :]
    own_score = (
        jnp.einsum("rhgd,rhd->rhg", query_srv, key_srv, preferred_element_type=jnp.float32)
        * score_scale
    )
    best = jnp.maximum(jnp.max(jnp.where(valid_pos, scores, -1e30), axis=(-2, -1)), own_score)
    weights = jnp.where(valid_pos, jnp.exp(scores - best[..., None, None]), 0.0)
    own_weight = jnp.exp(own_score - best)
    numer = (
        jnp.einsum("rhgpc,rphdc->rhgd", weights, value_rows.astype(jnp.float32))
        + own_weight[..., None] * value_srv.astype(jnp.float32)[:, :, None, :]
    )
    denom = jnp.sum(weights, axis=(-2, -1)) + own_weight
    attended = (numer / denom[..., None]).reshape(req_loc, q_loc * HEAD_SIZE).astype(jnp.bfloat16)

    summed = tensor_allreduce(
        jnp.dot(attended, w_output, preferred_element_type=jnp.float32), tp_count
    )
    mixed = rows_srv.astype(jnp.float32) + summed
    normed_mlp = norm_rows(mixed, mlp_gain).astype(jnp.bfloat16)
    gate_act = jnp.dot(normed_mlp, w_gate, preferred_element_type=jnp.float32)
    up_act = jnp.dot(normed_mlp, w_up, preferred_element_type=jnp.float32)
    hidden = (jax.nn.silu(gate_act) * up_act).astype(jnp.bfloat16)
    down_sum = tensor_allreduce(
        jnp.dot(hidden, w_down, preferred_element_type=jnp.float32), tp_count
    )
    final = (mixed + down_sum).astype(jnp.bfloat16)

    dest_rows = (
        jnp.arange(dp_count, dtype=jnp.int32)[:, None] * req_loc
        + tp_index * rows_loc
        + jnp.arange(rows_loc, dtype=jnp.int32)[None, :]
    ).reshape(-1)
    dest_round = jnp.sum(
        jnp.where(request_ids[None, :] == dest_rows[:, None], round_no[None, :], 0), axis=1
    )
    outgoing = final[dest_round.reshape(dp_count, rows_loc)]
    incoming = lax.all_to_all(outgoing, "dp", 0, 0)
    mine = dp_index * req_loc + tp_index * rows_loc + jnp.arange(rows_loc, dtype=jnp.int32)
    from_src = jnp.arange(dp_count, dtype=jnp.int32)[:, None] == server[mine][None, :]
    picked = jnp.where(from_src[:, :, None], incoming.astype(jnp.float32), 0.0)
    return jnp.sum(picked, axis=0).astype(jnp.bfloat16)


def solution(mesh):
    return jax.shard_map(
        local,
        mesh=mesh,
        in_specs=(
            P(("dp", "tensor"), None),
            P(),
            P(None, "tensor"),
            P(None, "tensor"),
            P(None, "tensor"),
            P("dp", "tensor", None, None),
            P("dp", "tensor", None, None),
            P(),
            P(),
            P("tensor", None),
            P(),
            P(None, "tensor"),
            P(None, "tensor"),
            P("tensor", None),
        ),
        out_specs=P(("dp", "tensor"), None),
        check_vma=False,
    )
```

```python
import jax
import jax.numpy as jnp
from jax import lax
from jax.sharding import PartitionSpec as P

HEAD_SIZE = 80


def norm_rows(value_rows, gain):
    value_rows = value_rows.astype(jnp.float32)
    return (
        value_rows
        * lax.rsqrt(jnp.mean(value_rows * value_rows, axis=-1, keepdims=True) + 1e-05)
        * gain.astype(jnp.float32)
    )


def apply_rotation(tensor, positions):
    half_dim = tensor.shape[-1] // 2
    inverse_freq = 1000000.0 ** (
        -(jnp.arange(half_dim, dtype=jnp.float32) * 2.0 / tensor.shape[-1])
    )
    angles = positions.astype(jnp.float32)[:, None] * inverse_freq[None, :]
    cosine = jnp.cos(angles)[:, None, :]
    sines = jnp.sin(angles)[:, None, :]
    first_half = tensor[..., :half_dim]
    second_half = tensor[..., half_dim:]
    return jnp.concatenate(
        [first_half * cosine - second_half * sines, second_half * cosine + first_half * sines],
        axis=-1,
    )


def tensor_allreduce(part, tp_count):
    def shifted(value, k):
        return lax.ppermute(value, "tensor", [(i, (i + k) % tp_count) for i in range(tp_count)])

    if tp_count == 4:
        return (part + shifted(part, 2)) + (shifted(part, 1) + shifted(part, 3))
    step = 1
    while step < tp_count:
        part = part + lax.ppermute(part, "tensor", [(i, i ^ step) for i in range(tp_count)])
        step *= 2
    return part


def local(
    residual_in,
    norm_gain,
    w_query,
    key_weight,
    value_weight,
    key_page_pool,
    value_page_pool,
    lengths,
    page_table,
    w_output,
    mlp_gain,
    w_gate,
    w_up,
    w_down,
):
    dp_count = lax.axis_size("dp")
    tp_count = lax.axis_size("tensor")
    rows_loc = residual_in.shape[0]
    req_loc = rows_loc * tp_count
    kv_loc = key_page_pool.shape[1]
    q_loc = w_query.shape[1] // HEAD_SIZE
    group_width = q_loc // kv_loc
    pool_size = key_page_pool.shape[0]
    page_len = key_page_pool.shape[3]
    per_req = page_table.shape[1]
    total_reqs = page_table.shape[0]
    score_scale = 1.0 / HEAD_SIZE**0.5
    dp_index = lax.axis_index("dp")
    tp_index = lax.axis_index("tensor")

    rows_dp = lax.all_to_all(
        jnp.broadcast_to(residual_in[None], (dp_count,) + residual_in.shape), "dp", 0, 0
    )

    request_ids = jnp.arange(total_reqs, dtype=jnp.int32)
    ranking = lengths * total_reqs + request_ids
    rank = jnp.sum((ranking[None, :] < ranking[:, None]).astype(jnp.int32), axis=1)
    round_no = rank // dp_count
    column = rank % dp_count
    server = jnp.where(round_no % 2 == 0, column, dp_count - 1 - column)
    slots = jnp.arange(req_loc, dtype=jnp.int32)
    hits = (server[None, :] == dp_index) & (round_no[None, :] == slots[:, None])
    served = jnp.sum(jnp.where(hits, request_ids[None, :], 0), axis=1)
    served_len = jnp.sum(jnp.where(hits, lengths[None, :], 0), axis=1)
    served_pages = jnp.sum(jnp.where(hits[:, :, None], page_table[None, :, :], 0), axis=1)

    owner_tp = (served % req_loc) // rows_loc
    held = rows_dp[served // req_loc, served % rows_loc]
    held = jnp.where((owner_tp == tp_index)[:, None], held, jnp.zeros_like(held))
    held, served_pages = lax.optimization_barrier((held, served_pages))
    rows_srv = held
    step = 1
    while step < tp_count:
        rows_srv = rows_srv + lax.ppermute(
            rows_srv, "tensor", [(i, i ^ step) for i in range(tp_count)]
        )
        step *= 2
    scaled_input = norm_rows(rows_srv, norm_gain).astype(jnp.bfloat16)
    query_srv = (
        apply_rotation(
            jnp.dot(scaled_input, w_query, preferred_element_type=jnp.float32).reshape(
                req_loc, q_loc, HEAD_SIZE
            ),
            served_len,
        )
        .astype(jnp.bfloat16)
        .reshape(req_loc, kv_loc, group_width, HEAD_SIZE)
    )
    key_srv = apply_rotation(
        jnp.dot(scaled_input, key_weight, preferred_element_type=jnp.float32).reshape(
            req_loc, kv_loc, HEAD_SIZE
        ),
        served_len,
    ).astype(jnp.bfloat16)
    value_srv = (
        jnp.dot(scaled_input, value_weight, preferred_element_type=jnp.float32)
        .astype(jnp.bfloat16)
        .reshape(req_loc, kv_loc, HEAD_SIZE)
    )

    page_list = (served_pages - dp_index * pool_size).reshape(-1)
    page_hot = (
        page_list[:, None] == jnp.arange(pool_size, dtype=jnp.int32)[None, :]
    ).astype(key_page_pool.dtype)
    key_rows = jnp.einsum(
        "sq,qhdc->shdc", page_hot, key_page_pool, preferred_element_type=jnp.bfloat16
    ).reshape((req_loc, per_req) + key_page_pool.shape[1:])
    value_rows = jnp.einsum(
        "sq,qhdc->shdc", page_hot, value_page_pool, preferred_element_type=jnp.bfloat16
    ).reshape((req_loc, per_req) + value_page_pool.shape[1:])
    scores = (
        jnp.einsum("rhgd,rphdc->rhgpc", query_srv, key_rows, preferred_element_type=jnp.float32)
        * score_scale
    )
    positions = (
        jnp.arange(per_req, dtype=jnp.int32)[:, None] * page_len
        + jnp.arange(page_len, dtype=jnp.int32)[None, :]
    )
    valid_pos = (positions[None, :, :] < served_len[:, None, None])[:, None, None, :, :]
    own_score = (
        jnp.einsum("rhgd,rhd->rhg", query_srv, key_srv, preferred_element_type=jnp.float32)
        * score_scale
    )
    best = jnp.maximum(jnp.max(jnp.where(valid_pos, scores, -1e30), axis=(-2, -1)), own_score)
    weights = jnp.where(valid_pos, jnp.exp(scores - best[..., None, None]), 0.0)
    own_weight = jnp.exp(own_score - best)
    numer = (
        jnp.einsum("rhgpc,rphdc->rhgd", weights, value_rows.astype(jnp.float32))
        + own_weight[..., None] * value_srv.astype(jnp.float32)[:, :, None, :]
    )
    denom = jnp.sum(weights, axis=(-2, -1)) + own_weight
    attended = (numer / denom[..., None]).reshape(req_loc, q_loc * HEAD_SIZE).astype(jnp.bfloat16)

    summed = tensor_allreduce(
        jnp.dot(attended, w_output, preferred_element_type=jnp.float32), tp_count
    )
    mixed = rows_srv.astype(jnp.float32) + summed
    normed_mlp = norm_rows(mixed, mlp_gain).astype(jnp.bfloat16)
    gate_act = jnp.dot(normed_mlp, w_gate, preferred_element_type=jnp.float32)
    up_act = jnp.dot(normed_mlp, w_up, preferred_element_type=jnp.float32)
    hidden = (jax.nn.silu(gate_act) * up_act).astype(jnp.bfloat16)
    down_sum = tensor_allreduce(
        jnp.dot(hidden, w_down, preferred_element_type=jnp.float32), tp_count
    )
    final = (mixed + down_sum).astype(jnp.bfloat16)

    dest_rows = (
        jnp.arange(dp_count, dtype=jnp.int32)[:, None] * req_loc
        + tp_index * rows_loc
        + jnp.arange(rows_loc, dtype=jnp.int32)[None, :]
    ).reshape(-1)
    dest_round = jnp.sum(
        jnp.where(request_ids[None, :] == dest_rows[:, None], round_no[None, :], 0), axis=1
    )
    outgoing = final[dest_round.reshape(dp_count, rows_loc)]
    incoming = lax.all_to_all(outgoing, "dp", 0, 0)
    mine = dp_index * req_loc + tp_index * rows_loc + jnp.arange(rows_loc, dtype=jnp.int32)
    from_src = jnp.arange(dp_count, dtype=jnp.int32)[:, None] == server[mine][None, :]
    picked = jnp.where(from_src[:, :, None], incoming.astype(jnp.float32), 0.0)
    return jnp.sum(picked, axis=0).astype(jnp.bfloat16)


def solution(mesh):
    return jax.shard_map(
        local,
        mesh=mesh,
        in_specs=(
            P(("dp", "tensor"), None),
            P(),
            P(None, "tensor"),
            P(None, "tensor"),
            P(None, "tensor"),
            P("dp", "tensor", None, None),
            P("dp", "tensor", None, None),
            P(),
            P(),
            P("tensor", None),
            P(),
            P(None, "tensor"),
            P(None, "tensor"),
            P("tensor", None),
        ),
        out_specs=P(("dp", "tensor"), None),
        check_vma=False,
    )
```

```python
import jax
import jax.numpy as jnp
from jax import lax
from jax.sharding import PartitionSpec as P

HEAD_SIZE = 80


def norm_rows(value_rows, gain):
    value_rows = value_rows.astype(jnp.float32)
    return (
        value_rows
        * lax.rsqrt(jnp.mean(value_rows * value_rows, axis=-1, keepdims=True) + 1e-05)
        * gain.astype(jnp.float32)
    )


def apply_rotation(tensor, positions):
    half_dim = tensor.shape[-1] // 2
    inverse_freq = 1000000.0 ** (
        -(jnp.arange(half_dim, dtype=jnp.float32) * 2.0 / tensor.shape[-1])
    )
    angles = positions.astype(jnp.float32)[:, None] * inverse_freq[None, :]
    cosine = jnp.cos(angles)[:, None, :]
    sines = jnp.sin(angles)[:, None, :]
    first_half = tensor[..., :half_dim]
    second_half = tensor[..., half_dim:]
    return jnp.concatenate(
        [first_half * cosine - second_half * sines, second_half * cosine + first_half * sines],
        axis=-1,
    )


def tensor_allreduce(part, tp_count):
    def shifted(value, k):
        return lax.ppermute(value, "tensor", [(i, (i + k) % tp_count) for i in range(tp_count)])

    if tp_count == 4:
        return (part + shifted(part, 2)) + (shifted(part, 1) + shifted(part, 3))
    step = 1
    while step < tp_count:
        part = part + lax.ppermute(part, "tensor", [(i, i ^ step) for i in range(tp_count)])
        step *= 2
    return part


def local(
    residual_in,
    norm_gain,
    w_query,
    key_weight,
    value_weight,
    key_page_pool,
    value_page_pool,
    lengths,
    page_table,
    w_output,
    mlp_gain,
    w_gate,
    w_up,
    w_down,
):
    dp_count = lax.axis_size("dp")
    tp_count = lax.axis_size("tensor")
    rows_loc = residual_in.shape[0]
    req_loc = rows_loc * tp_count
    kv_loc = key_page_pool.shape[1]
    q_loc = w_query.shape[1] // HEAD_SIZE
    group_width = q_loc // kv_loc
    pool_size = key_page_pool.shape[0]
    page_len = key_page_pool.shape[3]
    per_req = page_table.shape[1]
    total_reqs = page_table.shape[0]
    score_scale = 1.0 / HEAD_SIZE**0.5
    dp_index = lax.axis_index("dp")
    tp_index = lax.axis_index("tensor")

    width = residual_in.shape[1]
    sub = 8
    packed = residual_in.reshape(rows_loc * sub, width // sub)
    rows_dp = lax.all_to_all(
        jnp.broadcast_to(packed[None], (dp_count,) + packed.shape), "dp", 0, 0
    )

    request_ids = jnp.arange(total_reqs, dtype=jnp.int32)
    ranking = lengths * total_reqs + request_ids
    rank = jnp.sum((ranking[None, :] < ranking[:, None]).astype(jnp.int32), axis=1)
    round_no = rank // dp_count
    column = rank % dp_count
    server = jnp.where(round_no % 2 == 0, column, dp_count - 1 - column)
    slots = jnp.arange(req_loc, dtype=jnp.int32)
    hits = (server[None, :] == dp_index) & (round_no[None, :] == slots[:, None])
    served = jnp.sum(jnp.where(hits, request_ids[None, :], 0), axis=1)
    served_len = jnp.sum(jnp.where(hits, lengths[None, :], 0), axis=1)
    served_pages = jnp.sum(jnp.where(hits[:, :, None], page_table[None, :, :], 0), axis=1)

    owner_tp = (served % req_loc) // rows_loc
    sub_rows = (served % rows_loc)[:, None] * sub + jnp.arange(sub, dtype=jnp.int32)[None, :]
    held = rows_dp[(served // req_loc)[:, None], sub_rows].reshape(req_loc, width)
    held = jnp.where((owner_tp == tp_index)[:, None], held, jnp.zeros_like(held))
    held, served_pages = lax.optimization_barrier((held, served_pages))
    rows_srv = tensor_allreduce(held, tp_count)
    scaled_input = norm_rows(rows_srv, norm_gain).astype(jnp.bfloat16)
    query_srv = (
        apply_rotation(
            jnp.dot(scaled_input, w_query, preferred_element_type=jnp.float32).reshape(
                req_loc, q_loc, HEAD_SIZE
            ),
            served_len,
        )
        .astype(jnp.bfloat16)
        .reshape(req_loc, kv_loc, group_width, HEAD_SIZE)
    )
    key_srv = apply_rotation(
        jnp.dot(scaled_input, key_weight, preferred_element_type=jnp.float32).reshape(
            req_loc, kv_loc, HEAD_SIZE
        ),
        served_len,
    ).astype(jnp.bfloat16)
    value_srv = (
        jnp.dot(scaled_input, value_weight, preferred_element_type=jnp.float32)
        .astype(jnp.bfloat16)
        .reshape(req_loc, kv_loc, HEAD_SIZE)
    )

    page_list = (served_pages - dp_index * pool_size).reshape(-1)
    page_hot = (
        page_list[:, None] == jnp.arange(pool_size, dtype=jnp.int32)[None, :]
    ).astype(key_page_pool.dtype)
    key_rows = jnp.einsum(
        "sq,qhdc->shdc", page_hot, key_page_pool, preferred_element_type=jnp.bfloat16
    ).reshape((req_loc, per_req) + key_page_pool.shape[1:])
    value_rows = jnp.einsum(
        "sq,qhdc->shdc", page_hot, value_page_pool, preferred_element_type=jnp.bfloat16
    ).reshape((req_loc, per_req) + value_page_pool.shape[1:])
    scores = (
        jnp.einsum("rhgd,rphdc->rhgpc", query_srv, key_rows, preferred_element_type=jnp.float32)
        * score_scale
    )
    positions = (
        jnp.arange(per_req, dtype=jnp.int32)[:, None] * page_len
        + jnp.arange(page_len, dtype=jnp.int32)[None, :]
    )
    valid_pos = (positions[None, :, :] < served_len[:, None, None])[:, None, None, :, :]
    own_score = (
        jnp.einsum("rhgd,rhd->rhg", query_srv, key_srv, preferred_element_type=jnp.float32)
        * score_scale
    )
    best = jnp.maximum(jnp.max(jnp.where(valid_pos, scores, -1e30), axis=(-2, -1)), own_score)
    weights = jnp.where(valid_pos, jnp.exp(scores - best[..., None, None]), 0.0)
    own_weight = jnp.exp(own_score - best)
    numer = (
        jnp.einsum("rhgpc,rphdc->rhgd", weights, value_rows.astype(jnp.float32))
        + own_weight[..., None] * value_srv.astype(jnp.float32)[:, :, None, :]
    )
    denom = jnp.sum(weights, axis=(-2, -1)) + own_weight
    attended = (numer / denom[..., None]).reshape(req_loc, q_loc * HEAD_SIZE).astype(jnp.bfloat16)

    summed = tensor_allreduce(
        jnp.dot(attended, w_output, preferred_element_type=jnp.float32), tp_count
    )
    mixed = rows_srv.astype(jnp.float32) + summed
    normed_mlp = norm_rows(mixed, mlp_gain).astype(jnp.bfloat16)
    gate_act = jnp.dot(normed_mlp, w_gate, preferred_element_type=jnp.float32)
    up_act = jnp.dot(normed_mlp, w_up, preferred_element_type=jnp.float32)
    hidden = (jax.nn.silu(gate_act) * up_act).astype(jnp.bfloat16)
    down_sum = tensor_allreduce(
        jnp.dot(hidden, w_down, preferred_element_type=jnp.float32), tp_count
    )
    final = (mixed + down_sum).astype(jnp.bfloat16)

    dest_rows = (
        jnp.arange(dp_count, dtype=jnp.int32)[:, None] * req_loc
        + tp_index * rows_loc
        + jnp.arange(rows_loc, dtype=jnp.int32)[None, :]
    ).reshape(-1)
    dest_round = jnp.sum(
        jnp.where(request_ids[None, :] == dest_rows[:, None], round_no[None, :], 0), axis=1
    )
    outgoing = final[dest_round.reshape(dp_count, rows_loc)]
    incoming = lax.all_to_all(outgoing, "dp", 0, 0)
    mine = dp_index * req_loc + tp_index * rows_loc + jnp.arange(rows_loc, dtype=jnp.int32)
    from_src = jnp.arange(dp_count, dtype=jnp.int32)[:, None] == server[mine][None, :]
    picked = jnp.where(from_src[:, :, None], incoming.astype(jnp.float32), 0.0)
    return jnp.sum(picked, axis=0).astype(jnp.bfloat16)


def solution(mesh):
    return jax.shard_map(
        local,
        mesh=mesh,
        in_specs=(
            P(("dp", "tensor"), None),
            P(),
            P(None, "tensor"),
            P(None, "tensor"),
            P(None, "tensor"),
            P("dp", "tensor", None, None),
            P("dp", "tensor", None, None),
            P(),
            P(),
            P("tensor", None),
            P(),
            P(None, "tensor"),
            P(None, "tensor"),
            P("tensor", None),
        ),
        out_specs=P(("dp", "tensor"), None),
        check_vma=False,
    )
```

```python
import jax
import jax.numpy as jnp
from jax import lax
from jax.sharding import PartitionSpec as P

HEAD_SIZE = 80


def norm_rows(value_rows, gain):
    value_rows = value_rows.astype(jnp.float32)
    return (
        value_rows
        * lax.rsqrt(jnp.mean(value_rows * value_rows, axis=-1, keepdims=True) + 1e-05)
        * gain.astype(jnp.float32)
    )


def apply_rotation(tensor, positions):
    half_dim = tensor.shape[-1] // 2
    inverse_freq = 1000000.0 ** (
        -(jnp.arange(half_dim, dtype=jnp.float32) * 2.0 / tensor.shape[-1])
    )
    angles = positions.astype(jnp.float32)[:, None] * inverse_freq[None, :]
    cosine = jnp.cos(angles)[:, None, :]
    sines = jnp.sin(angles)[:, None, :]
    first_half = tensor[..., :half_dim]
    second_half = tensor[..., half_dim:]
    return jnp.concatenate(
        [first_half * cosine - second_half * sines, second_half * cosine + first_half * sines],
        axis=-1,
    )


def tensor_allreduce(part, tp_count):
    def shifted(value, k):
        return lax.ppermute(value, "tensor", [(i, (i + k) % tp_count) for i in range(tp_count)])

    if tp_count == 4:
        return (part + shifted(part, 2)) + (shifted(part, 1) + shifted(part, 3))
    step = 1
    while step < tp_count:
        part = part + lax.ppermute(part, "tensor", [(i, i ^ step) for i in range(tp_count)])
        step *= 2
    return part


def local(
    residual_in,
    norm_gain,
    w_query,
    key_weight,
    value_weight,
    key_page_pool,
    value_page_pool,
    lengths,
    page_table,
    w_output,
    mlp_gain,
    w_gate,
    w_up,
    w_down,
):
    dp_count = lax.axis_size("dp")
    tp_count = lax.axis_size("tensor")
    rows_loc = residual_in.shape[0]
    req_loc = rows_loc * tp_count
    kv_loc = key_page_pool.shape[1]
    q_loc = w_query.shape[1] // HEAD_SIZE
    group_width = q_loc // kv_loc
    pool_size = key_page_pool.shape[0]
    page_len = key_page_pool.shape[3]
    per_req = page_table.shape[1]
    total_reqs = page_table.shape[0]
    score_scale = 1.0 / HEAD_SIZE**0.5
    dp_index = lax.axis_index("dp")
    tp_index = lax.axis_index("tensor")

    rows_dp = lax.all_to_all(
        jnp.broadcast_to(residual_in[None], (dp_count,) + residual_in.shape), "dp", 0, 0
    )

    request_ids = jnp.arange(total_reqs, dtype=jnp.int32)
    ranking = lengths * total_reqs + request_ids
    rank = jnp.sum((ranking[None, :] < ranking[:, None]).astype(jnp.int32), axis=1)
    round_no = rank // dp_count
    column = rank % dp_count
    server = jnp.where(round_no % 2 == 0, column, dp_count - 1 - column)
    slots = jnp.arange(req_loc, dtype=jnp.int32)
    hits = (server[None, :] == dp_index) & (round_no[None, :] == slots[:, None])
    served = jnp.sum(jnp.where(hits, request_ids[None, :], 0), axis=1)
    served_len = jnp.sum(jnp.where(hits, lengths[None, :], 0), axis=1)
    served_pages = jnp.sum(jnp.where(hits[:, :, None], page_table[None, :, :], 0), axis=1)

    owner_tp = (served % req_loc) // rows_loc
    held = rows_dp[served // req_loc, served % rows_loc]
    held = jnp.where((owner_tp == tp_index)[:, None], held, jnp.zeros_like(held))
    held, served_pages = lax.optimization_barrier((held, served_pages))
    rows_srv = tensor_allreduce(held, tp_count)
    scaled_input = norm_rows(rows_srv, norm_gain).astype(jnp.bfloat16)
    query_srv = (
        apply_rotation(
            jnp.dot(scaled_input, w_query, preferred_element_type=jnp.float32).reshape(
                req_loc, q_loc, HEAD_SIZE
            ),
            served_len,
        )
        .astype(jnp.bfloat16)
        .reshape(req_loc, kv_loc, group_width, HEAD_SIZE)
    )
    key_srv = apply_rotation(
        jnp.dot(scaled_input, key_weight, preferred_element_type=jnp.float32).reshape(
            req_loc, kv_loc, HEAD_SIZE
        ),
        served_len,
    ).astype(jnp.bfloat16)
    value_srv = (
        jnp.dot(scaled_input, value_weight, preferred_element_type=jnp.float32)
        .astype(jnp.bfloat16)
        .reshape(req_loc, kv_loc, HEAD_SIZE)
    )

    page_list = (served_pages - dp_index * pool_size).reshape(-1)
    page_hot = (
        page_list[:, None] == jnp.arange(pool_size, dtype=jnp.int32)[None, :]
    ).astype(key_page_pool.dtype)
    key_rows = jnp.einsum(
        "sq,qhdc->shdc", page_hot, key_page_pool, preferred_element_type=jnp.bfloat16
    ).reshape((req_loc, per_req) + key_page_pool.shape[1:])
    value_rows = jnp.einsum(
        "sq,qhdc->shdc", page_hot, value_page_pool, preferred_element_type=jnp.bfloat16
    ).reshape((req_loc, per_req) + value_page_pool.shape[1:])
    scores = (
        jnp.einsum("rhgd,rphdc->rhgpc", query_srv, key_rows, preferred_element_type=jnp.float32)
        * score_scale
    )
    positions = (
        jnp.arange(per_req, dtype=jnp.int32)[:, None] * page_len
        + jnp.arange(page_len, dtype=jnp.int32)[None, :]
    )
    valid_pos = (positions[None, :, :] < served_len[:, None, None])[:, None, None, :, :]
    own_score = (
        jnp.einsum("rhgd,rhd->rhg", query_srv, key_srv, preferred_element_type=jnp.float32)
        * score_scale
    )
    best = jnp.maximum(jnp.max(jnp.where(valid_pos, scores, -1e30), axis=(-2, -1)), own_score)
    weights = jnp.where(valid_pos, jnp.exp(scores - best[..., None, None]), 0.0)
    own_weight = jnp.exp(own_score - best)
    numer = (
        jnp.einsum("rhgpc,rphdc->rhgd", weights, value_rows.astype(jnp.float32))
        + own_weight[..., None] * value_srv.astype(jnp.float32)[:, :, None, :]
    )
    denom = jnp.sum(weights, axis=(-2, -1)) + own_weight
    attended = (numer / denom[..., None]).reshape(req_loc, q_loc * HEAD_SIZE).astype(jnp.bfloat16)

    summed = tensor_allreduce(
        jnp.dot(attended, w_output, preferred_element_type=jnp.float32), tp_count
    )
    mixed = rows_srv.astype(jnp.float32) + summed
    normed_mlp = norm_rows(mixed, mlp_gain).astype(jnp.bfloat16)
    gate_act = jnp.dot(normed_mlp, w_gate, preferred_element_type=jnp.float32)
    up_act = jnp.dot(normed_mlp, w_up, preferred_element_type=jnp.float32)
    hidden = (jax.nn.silu(gate_act) * up_act).astype(jnp.bfloat16)
    down_sum = tensor_allreduce(
        jnp.dot(hidden, w_down, preferred_element_type=jnp.float32), tp_count
    )
    final = (mixed + down_sum).astype(jnp.bfloat16)

    dest_rows = (
        jnp.arange(dp_count, dtype=jnp.int32)[:, None] * req_loc
        + tp_index * rows_loc
        + jnp.arange(rows_loc, dtype=jnp.int32)[None, :]
    ).reshape(-1)
    gathered = lax.all_gather(final, "dp")
    mine = dp_index * req_loc + tp_index * rows_loc + jnp.arange(rows_loc, dtype=jnp.int32)
    own_hot = (jnp.arange(dp_count, dtype=jnp.int32)[None, :, None] == server[mine][:, None, None]) & (
        slots[None, None, :] == round_no[mine][:, None, None]
    )
    picked = jnp.where(own_hot[..., None], gathered.astype(jnp.float32)[None], 0.0)
    return jnp.sum(picked, axis=(1, 2)).astype(jnp.bfloat16)


def solution(mesh):
    return jax.shard_map(
        local,
        mesh=mesh,
        in_specs=(
            P(("dp", "tensor"), None),
            P(),
            P(None, "tensor"),
            P(None, "tensor"),
            P(None, "tensor"),
            P("dp", "tensor", None, None),
            P("dp", "tensor", None, None),
            P(),
            P(),
            P("tensor", None),
            P(),
            P(None, "tensor"),
            P(None, "tensor"),
            P("tensor", None),
        ),
        out_specs=P(("dp", "tensor"), None),
        check_vma=False,
    )
```

```python
import jax
import jax.numpy as jnp
from jax import lax
from jax.sharding import PartitionSpec as P

HEAD_SIZE = 80


def norm_rows(value_rows, gain):
    value_rows = value_rows.astype(jnp.float32)
    return (
        value_rows
        * lax.rsqrt(jnp.mean(value_rows * value_rows, axis=-1, keepdims=True) + 1e-05)
        * gain.astype(jnp.float32)
    )


def apply_rotation(tensor, positions):
    half_dim = tensor.shape[-1] // 2
    inverse_freq = 1000000.0 ** (
        -(jnp.arange(half_dim, dtype=jnp.float32) * 2.0 / tensor.shape[-1])
    )
    angles = positions.astype(jnp.float32)[:, None] * inverse_freq[None, :]
    cosine = jnp.cos(angles)[:, None, :]
    sines = jnp.sin(angles)[:, None, :]
    first_half = tensor[..., :half_dim]
    second_half = tensor[..., half_dim:]
    return jnp.concatenate(
        [first_half * cosine - second_half * sines, second_half * cosine + first_half * sines],
        axis=-1,
    )


def tensor_allreduce(part, tp_count):
    def shifted(value, k):
        return lax.ppermute(value, "tensor", [(i, (i + k) % tp_count) for i in range(tp_count)])

    if tp_count == 4:
        return (part + shifted(part, 2)) + (shifted(part, 1) + shifted(part, 3))
    step = 1
    while step < tp_count:
        part = part + lax.ppermute(part, "tensor", [(i, i ^ step) for i in range(tp_count)])
        step *= 2
    return part


def local(
    residual_in,
    norm_gain,
    w_query,
    key_weight,
    value_weight,
    key_page_pool,
    value_page_pool,
    lengths,
    page_table,
    w_output,
    mlp_gain,
    w_gate,
    w_up,
    w_down,
):
    dp_count = lax.axis_size("dp")
    tp_count = lax.axis_size("tensor")
    rows_loc = residual_in.shape[0]
    req_loc = rows_loc * tp_count
    kv_loc = key_page_pool.shape[1]
    q_loc = w_query.shape[1] // HEAD_SIZE
    group_width = q_loc // kv_loc
    pool_size = key_page_pool.shape[0]
    page_len = key_page_pool.shape[3]
    per_req = page_table.shape[1]
    total_reqs = page_table.shape[0]
    score_scale = 1.0 / HEAD_SIZE**0.5
    dp_index = lax.axis_index("dp")
    tp_index = lax.axis_index("tensor")

    rows_dp = lax.all_gather(residual_in, "dp")

    request_ids = jnp.arange(total_reqs, dtype=jnp.int32)
    ranking = lengths * total_reqs + request_ids
    rank = jnp.sum((ranking[None, :] < ranking[:, None]).astype(jnp.int32), axis=1)
    round_no = rank // dp_count
    column = rank % dp_count
    server = jnp.where(round_no % 2 == 0, column, dp_count - 1 - column)
    slots = jnp.arange(req_loc, dtype=jnp.int32)
    hits = (server[None, :] == dp_index) & (round_no[None, :] == slots[:, None])
    served = jnp.sum(jnp.where(hits, request_ids[None, :], 0), axis=1)
    served_len = jnp.sum(jnp.where(hits, lengths[None, :], 0), axis=1)
    served_pages = jnp.sum(jnp.where(hits[:, :, None], page_table[None, :, :], 0), axis=1)

    owner_tp = (served % req_loc) // rows_loc
    held = rows_dp[served // req_loc, served % rows_loc]
    held = jnp.where((owner_tp == tp_index)[:, None], held, jnp.zeros_like(held))
    held, served_pages = lax.optimization_barrier((held, served_pages))
    rows_srv = tensor_allreduce(held, tp_count)
    scaled_input = norm_rows(rows_srv, norm_gain).astype(jnp.bfloat16)
    query_srv = (
        apply_rotation(
            jnp.dot(scaled_input, w_query, preferred_element_type=jnp.float32).reshape(
                req_loc, q_loc, HEAD_SIZE
            ),
            served_len,
        )
        .astype(jnp.bfloat16)
        .reshape(req_loc, kv_loc, group_width, HEAD_SIZE)
    )
    key_srv = apply_rotation(
        jnp.dot(scaled_input, key_weight, preferred_element_type=jnp.float32).reshape(
            req_loc, kv_loc, HEAD_SIZE
        ),
        served_len,
    ).astype(jnp.bfloat16)
    value_srv = (
        jnp.dot(scaled_input, value_weight, preferred_element_type=jnp.float32)
        .astype(jnp.bfloat16)
        .reshape(req_loc, kv_loc, HEAD_SIZE)
    )

    page_list = (served_pages - dp_index * pool_size).reshape(-1)
    page_hot = (
        page_list[:, None] == jnp.arange(pool_size, dtype=jnp.int32)[None, :]
    ).astype(key_page_pool.dtype)
    key_rows = jnp.einsum(
        "sq,qhdc->shdc", page_hot, key_page_pool, preferred_element_type=jnp.bfloat16
    ).reshape((req_loc, per_req) + key_page_pool.shape[1:])
    value_rows = jnp.einsum(
        "sq,qhdc->shdc", page_hot, value_page_pool, preferred_element_type=jnp.bfloat16
    ).reshape((req_loc, per_req) + value_page_pool.shape[1:])
    scores = (
        jnp.einsum("rhgd,rphdc->rhgpc", query_srv, key_rows, preferred_element_type=jnp.float32)
        * score_scale
    )
    positions = (
        jnp.arange(per_req, dtype=jnp.int32)[:, None] * page_len
        + jnp.arange(page_len, dtype=jnp.int32)[None, :]
    )
    valid_pos = (positions[None, :, :] < served_len[:, None, None])[:, None, None, :, :]
    own_score = (
        jnp.einsum("rhgd,rhd->rhg", query_srv, key_srv, preferred_element_type=jnp.float32)
        * score_scale
    )
    best = jnp.maximum(jnp.max(jnp.where(valid_pos, scores, -1e30), axis=(-2, -1)), own_score)
    weights = jnp.where(valid_pos, jnp.exp(scores - best[..., None, None]), 0.0)
    own_weight = jnp.exp(own_score - best)
    numer = (
        jnp.einsum("rhgpc,rphdc->rhgd", weights, value_rows.astype(jnp.float32))
        + own_weight[..., None] * value_srv.astype(jnp.float32)[:, :, None, :]
    )
    denom = jnp.sum(weights, axis=(-2, -1)) + own_weight
    attended = (numer / denom[..., None]).reshape(req_loc, q_loc * HEAD_SIZE).astype(jnp.bfloat16)

    summed = tensor_allreduce(
        jnp.dot(attended, w_output, preferred_element_type=jnp.float32), tp_count
    )
    mixed = rows_srv.astype(jnp.float32) + summed
    normed_mlp = norm_rows(mixed, mlp_gain).astype(jnp.bfloat16)
    gate_act = jnp.dot(normed_mlp, w_gate, preferred_element_type=jnp.float32)
    up_act = jnp.dot(normed_mlp, w_up, preferred_element_type=jnp.float32)
    hidden = (jax.nn.silu(gate_act) * up_act).astype(jnp.bfloat16)
    down_sum = tensor_allreduce(
        jnp.dot(hidden, w_down, preferred_element_type=jnp.float32), tp_count
    )
    final = (mixed + down_sum).astype(jnp.bfloat16)

    dest_rows = (
        jnp.arange(dp_count, dtype=jnp.int32)[:, None] * req_loc
        + tp_index * rows_loc
        + jnp.arange(rows_loc, dtype=jnp.int32)[None, :]
    ).reshape(-1)
    gathered = lax.all_gather(final, "dp")
    mine = dp_index * req_loc + tp_index * rows_loc + jnp.arange(rows_loc, dtype=jnp.int32)
    own_hot = (jnp.arange(dp_count, dtype=jnp.int32)[None, :, None] == server[mine][:, None, None]) & (
        slots[None, None, :] == round_no[mine][:, None, None]
    )
    picked = jnp.where(own_hot[..., None], gathered.astype(jnp.float32)[None], 0.0)
    return jnp.sum(picked, axis=(1, 2)).astype(jnp.bfloat16)


def solution(mesh):
    return jax.shard_map(
        local,
        mesh=mesh,
        in_specs=(
            P(("dp", "tensor"), None),
            P(),
            P(None, "tensor"),
            P(None, "tensor"),
            P(None, "tensor"),
            P("dp", "tensor", None, None),
            P("dp", "tensor", None, None),
            P(),
            P(),
            P("tensor", None),
            P(),
            P(None, "tensor"),
            P(None, "tensor"),
            P("tensor", None),
        ),
        out_specs=P(("dp", "tensor"), None),
        check_vma=False,
    )
```
